128 devices in a mesh: seq: 16 (over y, z), row: 2 (over core), col: 4 (over x).
Axes of the slice: x: 4, y: 4, z: 4, core: 2. Of those that a mesh axis runs over, the one named last changes fastest.
Arguments:
- hidden_in: bfloat16 [256, 1536], P('seq'), may hold values from -40 to 40
- attn_gain: float32 [1536], replicated, may hold values from 0.25 to 1.75
- w_query: bfloat16 [1536, 1536], P('seq', ('row', 'col')), may hold values from -0.15625 to 0.15625
- w_keyval: bfloat16 [1536, 1024], P('seq', ('row', 'col')), may hold values from -0.15625 to 0.15625
- w_out: bfloat16 [1536, 1536], P(('row', 'col'), 'seq'), may hold values from -0.15625 to 0.15625
- kv_cache: bfloat16 [64, 24576, 1024], P(None, 'seq', ('row', 'col')), may hold values from -360 to 360
- cache_len: int32 [64], replicated, may hold values from 1 to 24576, as said below
- ffn_gain: float32 [1536], replicated, may hold values from 0.25 to 1.75
- w_router: float32 [1536, 16], replicated, may hold values from -0.15625 to 0.15625
- routes: int32 [256, 2], replicated, may hold values from 0 to 15, all different within a row; in each aligned block of 256 rows (0 to 255, 256 to 511, ...) at most 64 rows name the same one
- w_gate_up: bfloat16 [16, 1536, 2, 1024], P('seq', 'row', None, 'col'), may hold values from -0.15625 to 0.15625
- w_down: bfloat16 [16, 1024, 1536], P('seq', 'col', 'row'), may hold values from -0.1875 to 0.1875
- final_gain: float32 [1536], replicated, may hold values from 0.25 to 1.75
- w_head: bfloat16 [1536, 65536], P('row', ('seq', 'col')), may hold values from -1.75 to 1.75
- targets: int32 [256], replicated, may hold values from 0 to 65535
Outputs:
- layer_out: bfloat16 [256, 1536], P(('seq', 'col'), 'row')
- logprob: float32 [256], replicated
The draws below stay inside these ranges and needn't reach their ends.
Inputs may be any that keep to these rules, and one draw needn't show every extreme that they name: `cache_len`: lengths are uneven; some request has exactly 24576 cached positions. `routes`: the two experts of a row differ; each expert is named by at most 64 rows, a bound that some block reaches.
All inputs are finite; a program needn't handle non-finite values.
Results may differ from the reference program's by a relative error of at most 0.0044.
Values may be sent and summed in bfloat16 or wider, within the bound.
No kernel may reach another device: no remote copies, remote signals or barrier semaphores. Data moves between devices by JAX's collectives and lax.ppermute only.
A program may use at most 128 MiB of HBM per device.

```python
import math
import jax
import jax.numpy as jnp
import numpy as np
from jax import lax

D = 1536
HEADS = 24
KVH = 8
HD = 64
FF = 1024
VOCAB = 65536
TOP = 2
NEW = 4
REQ = 64
EXPERTS = 16
NQ = 256
LMAX = 24576
GROUP = 3
CAP = 64


def draw_hidden_in(key, part):
    key_a = jax.random.fold_in(key, 0)
    columns = jnp.arange(D, dtype=jnp.float32) / (D - 1)
    base = jnp.clip(jax.random.normal(key_a, (NQ, D), jnp.float32), -6.0, 6.0)
    column_scale = 0.5 * jnp.exp(columns * math.log(6.0))
    table = base * column_scale[None, :]
    return jnp.clip(table, -40.0, 40.0).astype(jnp.bfloat16)


def draw_cache_len(key, part):
    first_key, second_key, third_key, fourth_key, fifth_key = jax.random.split(key, 5)
    first = jax.random.randint(first_key, (REQ,), 1, LMAX + 1)
    second = jax.random.randint(second_key, (REQ,), 1, LMAX + 1)
    lengths = jnp.maximum(first, second)
    short_top = min(32, LMAX)
    short = jax.random.randint(fourth_key, (REQ,), 1, short_top + 1)
    picked = jax.random.randint(fifth_key, (REQ,), 0, 4) == 0
    lengths = jnp.where(picked, short, lengths)
    longest = jax.random.randint(third_key, (), 0, REQ)
    return lengths.at[longest].set(LMAX).astype(jnp.int32)


def draw_kv_cache(key, part):
    key_a = jax.random.fold_in(key, 0)
    key_b = jax.random.fold_in(key, 1)
    key_e = jax.random.fold_in(key, 4)
    value_part = jnp.clip(jax.random.normal(key_b, (REQ, LMAX, KVH, 1, HD), jnp.float32), -6.0, 6.0)
    signs = jnp.where(jax.random.uniform(key_e, (1, 1, KVH, 1, HD), jnp.float32) < 0.5, -1.0, 1.0)
    along = (jnp.arange(LMAX, dtype=jnp.float32) / (LMAX - 1)).reshape(1, LMAX, 1, 1, 1)
    drift = 0.2 + 1.3 * along
    key_part = jnp.clip(jax.random.normal(key_a, (REQ, LMAX, KVH, 1, HD), jnp.float32), -6.0, 6.0)
    value_part = value_part + drift * signs
    joined = jnp.concatenate([key_part, value_part], axis=3)
    return joined.reshape(REQ, LMAX, KVH * 2 * HD).astype(jnp.bfloat16)


def draw_w_head(key, part):
    key_a = jax.random.fold_in(key, 0)
    table = jnp.clip(jax.random.normal(key_a, (D, VOCAB), jnp.float32), -6.0, 6.0) * D ** (-0.5)
    return jnp.clip(table, -1.75, 1.75).astype(jnp.bfloat16)


def place_ends(values, rng, least, largest):
    index_at = [jax.random.randint(jax.random.fold_in(rng, axis), (), 0, length) for axis, length in enumerate(values.shape)]
    widest = values.shape.index(max(values.shape))
    beside = index_at[:widest] + [(index_at[widest] + 1) % values.shape[widest]] + index_at[widest + 1:]
    return values.at[tuple(index_at)].set(least).at[tuple(beside)].set(largest)


def block_scale(stream_key, shape, cuts, smallest, high):
    def one(axis_at, parts):
        steps = jax.random.uniform(jax.random.fold_in(jax.random.fold_in(stream_key, 6), axis_at), (parts,), jnp.float32, smallest / len(cuts), high / len(cuts))
        return jnp.repeat(jnp.exp(steps), shape[axis_at] // parts).reshape((-1,) + (1,) * (len(shape) - axis_at - 1))

    factor_of = one(*cuts[0])
    for cut in cuts[1:]:
        factor_of = factor_of * one(*cut)
    return factor_of


def rank_bounds(number_of, skew):
    portions = [(1 << 20) // math.isqrt(standing ** skew) + 1 for standing in range(1, number_of + 1)]
    width = 1 + sum(portions) // (1 << 30)
    return np.cumsum(np.array([max(1, weight // width) for weight in portions]))


def ranked_ids(stream_key, dims, count, skew):
    listing = rank_bounds(count, skew)
    lot = jax.random.randint(jax.random.fold_in(stream_key, 1), dims, 0, int(listing[count - 1]))
    standing = jnp.searchsorted(jnp.asarray(listing, jnp.int32), lot, side="right")
    return jax.random.permutation(jax.random.fold_in(stream_key, 2), count)[standing].astype(jnp.int32)


def assign_block(rng, own, number, rows, count, top, reach, lean):
    order = jax.random.permutation(rng, count)
    packed, common = load_shares(count, rows * top, reach, lean, True), load_shares(count, rows * top, reach, lean, False)
    places = jnp.arange(count)

    def named(sizes, turn):
        used = int((sizes > 0).sum())
        fixed = max(1, used // 4)
        moved = fixed + (places - fixed + turn * (used - fixed)) % max(1, count - fixed)
        return jnp.zeros((count,), jnp.int32).at[order[jnp.where(places < fixed, places, moved)]].set(jnp.asarray(sizes, jnp.int32))

    sizes = jnp.where(number % 4 == 0, named(packed, number // 4), named(common, number - number // 4 - 1))
    mixed = jax.random.permutation(jax.random.fold_in(own, 3), count)
    source_of, receiver = mixed[0:count // 2 * 2:2], mixed[1:count // 2 * 2:2]
    slack = jnp.minimum(sizes[source_of] - 1, reach - sizes[receiver]) // 2
    slack = jnp.where((source_of == order[0]) | (receiver == order[0]) | (sizes[receiver] == 0), 0, jnp.maximum(slack, 0))
    moved = jax.random.randint(jax.random.fold_in(own, 4), (count // 2,), 0, 1 << 20) % (slack + 1)
    sizes = sizes.at[source_of].add(-moved).at[receiver].add(moved)
    members = jnp.searchsorted(jnp.cumsum(sizes), jnp.arange(rows * top), side="right").astype(jnp.int32)
    grid = members.reshape(top, rows).T
    grid = grid[jax.random.permutation(jax.random.fold_in(own, 1), rows)]
    turn = jax.random.randint(jax.random.fold_in(own, 2), (rows, 1), 0, top)
    return jnp.take_along_axis(grid, (jnp.arange(top)[None, :] + turn) % top, axis=1)


def load_shares(amount, total, bound, skew, full):
    portions = [(1 << 20) // math.isqrt(rank ** skew) + 1 for rank in range(1, amount + 1)]
    largest = bound if full else min(bound, max(-(-total // amount), total * portions[0] // sum(portions)))
    least = 1 if total - largest >= amount - 1 else 0
    given, spare = [largest] + [least] * (amount - 1), total - largest - least * (amount - 1)
    while spare > 0:
        free = [i for i in range(1, amount) if given[i] < largest] or [i for i in range(1, amount) if given[i] < bound]
        pool, remaining = sum([portions[i] for i in free]), spare
        for i in free:
            more = min(bound - given[i], max(1, remaining * portions[i] // pool), spare)
            given[i] = given[i] + more
            spare = spare - more
    return np.array(given)


def centred(stream_key, extent, width, bound, cuts=(), kind=jnp.bfloat16):
    values = jax.random.normal(stream_key, extent, jnp.float32) * width
    if len(cuts) > 0:
        values = block_scale(stream_key, extent, cuts, -0.22, 0.18) * values
    return jnp.clip(values, min=-bound, max=bound).astype(kind)


def setup_inputs(seed: int = 0) -> dict:
    key_of = jax.random.split(jax.random.key(seed), 16)
    hidden_in = draw_hidden_in(jax.random.fold_in(key_of[15], 71), 0)
    attn_gain = jnp.clip(1.0 + 0.15 * jax.random.normal(key_of[1], (D,), jnp.float32), 0.25, 1.75)
    w_query = centred(key_of[2], (D, HEADS * HD), D ** -0.5, 0.15625, ((0, 16), (1, 8)))
    w_keyval = centred(key_of[3], (D, KVH * 2 * HD), D ** -0.5, 0.15625, ((0, 16), (1, 8)))
    w_out = centred(key_of[4], (HEADS * HD, D), (HEADS * HD) ** -0.5, 0.15625, ((0, 8), (1, 16)))
    kv_cache = draw_kv_cache(jax.random.fold_in(key_of[15], 71), 0)
    cache_len = draw_cache_len(jax.random.fold_in(key_of[15], 71), 0)
    ffn_gain = jnp.clip(1.0 + 0.15 * jax.random.normal(key_of[7], (D,), jnp.float32), 0.25, 1.75)
    w_router = centred(key_of[8], (D, EXPERTS), D ** -0.5, 0.15625, (), jnp.float32)
    routes_keys = jax.random.split(jax.random.fold_in(key_of[9], 1), NQ // NQ)
    routes_turns = jax.random.permutation(jax.random.fold_in(key_of[9], 3), NQ // NQ)
    routes = jax.vmap(lambda own, number: assign_block(jax.random.fold_in(key_of[9], 2), own, number, NQ, EXPERTS, TOP, CAP, 2))(routes_keys, routes_turns).reshape((NQ, TOP))
    w_gate_up = centred(key_of[10], (EXPERTS, D, 2, FF), D ** -0.5, 0.15625, ((0, 16), (1, 2), (3, 4)))
    w_down = centred(key_of[11], (EXPERTS, FF, D), FF ** -0.5, 0.1875, ((0, 16), (1, 4), (2, 2)))
    final_gain = jnp.clip(1.0 + 0.15 * jax.random.normal(key_of[12], (D,), jnp.float32), 0.25, 1.75)
    w_head = draw_w_head(jax.random.fold_in(key_of[15], 71), 0)
    targets = place_ends(ranked_ids(key_of[14], (NQ,), VOCAB, 2), jax.random.fold_in(key_of[14], 3), 0, VOCAB - 1).astype(jnp.int32)
    return dict(hidden_in=hidden_in, attn_gain=attn_gain, w_query=w_query, w_keyval=w_keyval, w_out=w_out, kv_cache=kv_cache, cache_len=cache_len, ffn_gain=ffn_gain, w_router=w_router, routes=routes, w_gate_up=w_gate_up, w_down=w_down, final_gain=final_gain, w_head=w_head, targets=targets)


EPSILON = 1e-05

def rms_scale(values, gain):
    mean_square = lax.optimization_barrier(jnp.mean(values * values, axis=-1, keepdims=True))
    return values * lax.rsqrt(mean_square + EPSILON) * gain

def attend_request(items):
    query_rows, cached, fresh, length = items
    scale = HD ** (-0.5)
    cached_keys = cached[:, :, 0].astype(jnp.float32)
    cached_values = cached[:, :, 1].astype(jnp.float32)
    fresh_keys = fresh[:, :, 0].astype(jnp.float32)
    fresh_values = fresh[:, :, 1].astype(jnp.float32)
    old_scores = jnp.einsum('tkgd,pkd->kgtp', query_rows, cached_keys, precision=lax.Precision.HIGHEST) * scale
    new_scores = jnp.einsum('tkgd,ukd->kgtu', query_rows, fresh_keys, precision=lax.Precision.HIGHEST) * scale
    old_mask = (jnp.arange(LMAX, dtype=jnp.int32) < length)[None, None, None, :]
    new_mask = (jnp.arange(NEW)[:, None] >= jnp.arange(NEW)[None, :])[None, None]
    old_scores = jnp.where(old_mask, old_scores, -jnp.inf)
    new_scores = jnp.where(new_mask, new_scores, -jnp.inf)
    highest = jnp.maximum(lax.optimization_barrier(jnp.max(old_scores, axis=-1)), lax.optimization_barrier(jnp.max(new_scores, axis=-1)))
    old_weights = jnp.exp(old_scores - highest[..., None])
    new_weights = jnp.exp(new_scores - highest[..., None])
    totals = old_weights.sum(-1) + new_weights.sum(-1)
    mixed = jnp.einsum('kgtp,pkd->tkgd', old_weights, cached_values, precision=lax.Precision.HIGHEST)
    mixed = mixed + jnp.einsum('kgtu,ukd->tkgd', new_weights, fresh_values, precision=lax.Precision.HIGHEST)
    return mixed / jnp.transpose(totals, (2, 0, 1))[..., None]

def reference(hidden_in, attn_gain, w_query, w_keyval, w_out, kv_cache, cache_len, ffn_gain, w_router, routes, w_gate_up, w_down, final_gain, w_head, targets):
    state_in = hidden_in.astype(jnp.float32)
    normed_in = rms_scale(state_in, attn_gain).astype(jnp.bfloat16)
    query = jnp.dot(normed_in, w_query, preferred_element_type=jnp.float32)
    fresh_kv = jnp.dot(normed_in, w_keyval, preferred_element_type=jnp.float32).astype(jnp.bfloat16)
    query_rows = query.reshape(REQ, NEW, KVH, GROUP, HD)
    fresh_rows = fresh_kv.reshape(REQ, NEW, KVH, 2, HD)
    cached = kv_cache.reshape(REQ, LMAX, KVH, 2, HD)
    mixed = lax.map(attend_request, (query_rows, cached, fresh_rows, cache_len))
    attn_mix = mixed.reshape(NQ, HEADS * HD).astype(jnp.bfloat16)
    state_mid = state_in + jnp.dot(attn_mix, w_out, preferred_element_type=jnp.float32)
    normed_mid = rms_scale(state_mid, ffn_gain).astype(jnp.bfloat16)
    router = jnp.dot(normed_mid.astype(jnp.float32), w_router, precision=lax.Precision.HIGHEST)
    chosen = jnp.take_along_axis(router, routes, axis=1)
    probs = jax.nn.sigmoid(chosen - chosen[:, ::-1])
    row_ids = jnp.arange(NQ, dtype=jnp.int32)

    def expert_step(carry, items):
        expert, gate_up, down = items
        member = routes == expert
        in_row = jnp.any(member, axis=1)
        weight_row = lax.optimization_barrier(jnp.sum(jnp.where(member, probs, 0.0), axis=1))
        order = jnp.cumsum(in_row.astype(jnp.int32)) - 1
        filled = jnp.sum(in_row.astype(jnp.int32))
        source = jnp.zeros((CAP,), jnp.int32).at[jnp.where(in_row, order, CAP)].set(row_ids, mode='drop')
        active = jnp.arange(CAP, dtype=jnp.int32) < filled
        gathered = normed_mid[source]
        both = jnp.dot(gathered, gate_up.reshape(D, 2 * FF), preferred_element_type=jnp.float32).reshape(CAP, 2, FF)
        expert_hidden = (jax.nn.silu(both[:, 0]) * both[:, 1]).astype(jnp.bfloat16)
        result = jnp.dot(expert_hidden, down, preferred_element_type=jnp.float32)
        result = result * jnp.where(active, weight_row[source], 0.0)[:, None]
        return (carry.at[source].add(result), None)
    mixture, _ = lax.scan(expert_step, jnp.zeros((NQ, D), jnp.float32), (jnp.arange(EXPERTS, dtype=jnp.int32), w_gate_up, w_down))
    state_out = state_mid + mixture
    layer_out = state_out.astype(jnp.bfloat16)
    normed_out = rms_scale(state_out, final_gain).astype(jnp.bfloat16)
    logits = jnp.dot(normed_out, w_head, preferred_element_type=jnp.float32)
    highest = lax.optimization_barrier(jnp.max(logits, axis=1))
    log_total = jnp.log(lax.optimization_barrier(jnp.sum(jnp.exp(logits - highest[:, None]), axis=1)))
    picked = jnp.take_along_axis(logits, targets[:, None], axis=1)[:, 0]
    logprob = picked - (highest + log_total)
    return (layer_out, logprob)
```

```python
import jax
import jax.numpy as jnp
from jax import lax
from jax.sharding import PartitionSpec as P

HD = 64
EXP_DEV = 1
TOP = 2
NEW = 4


EPSILON = 1e-05
NEG_LARGE = -1e30


def combined_all(shard, axis, combine):
    everything = jax.tree.map(lambda part: lax.all_gather(part, axis), shard)
    initial = jax.tree.map(lambda part: part[0], everything)

    def lap(k, so_far):
        return combine(so_far, jax.tree.map(lambda part: part[k], everything))

    return lax.fori_loop(1, lax.axis_size(axis), lap, initial)


def butterfly_merge(value, axes, count, combine):
    step = 1
    while step < count:
        pairs = [(i, i ^ step) for i in range(count)]
        other = jax.tree.map(lambda part: lax.ppermute(part, axes, pairs), value)
        value = combine(value, other)
        step *= 2
    return value


def halving_scatter(value, axes, count):
    index = lax.axis_index(axes)
    step = count // 2
    while step >= 1:
        half = value.shape[0] // 2
        upper = (index // step) % 2 == 1
        low, high = value[:half], value[half:]
        send = jnp.where(upper, low, high)
        keep = jnp.where(upper, high, low)
        pairs = [(i, i ^ step) for i in range(count)]
        value = keep + lax.ppermute(send, axes, pairs)
        step //= 2
    return value


def doubling_gather(value, axes, count):
    index = lax.axis_index(axes)
    step = 1
    while step < count:
        upper = (index // step) % 2 == 1
        pairs = [(i, i ^ step) for i in range(count)]
        other = lax.ppermute(value, axes, pairs)
        value = jnp.where(
            upper, jnp.concatenate([other, value]), jnp.concatenate([value, other])
        )
        step *= 2
    return value


def merge_logsumexp(first, second):
    high_a, sums_a, picked_a = first
    high_b, sums_b, picked_b = second
    highest = jnp.maximum(high_a, high_b)
    return (
        highest,
        sums_a * jnp.exp(high_a - highest) + sums_b * jnp.exp(high_b - highest),
        picked_a + picked_b,
    )


def rms_scale(values, gain):
    mean_square = jnp.mean(values * values, axis=-1, keepdims=True)
    return values * lax.rsqrt(mean_square + EPSILON) * gain


def final_scale(state, gain_half, width):
    squares = lax.psum(jnp.sum(state * state, axis=-1), "row")
    return (state * lax.rsqrt(squares[:, None] / width + EPSILON) * gain_half).astype(jnp.bfloat16)


def merge_softmax(first, second):
    high_a, sums_a, mixed_a = first
    high_b, sums_b, mixed_b = second
    highest = jnp.maximum(high_a, high_b)
    factor_a = jnp.exp(high_a - highest)
    factor_b = jnp.exp(high_b - highest)
    shaped_a = mixed_a.reshape(highest.shape + (-1,)) * factor_a[..., None]
    shaped_b = mixed_b.reshape(highest.shape + (-1,)) * factor_b[..., None]
    return (
        highest,
        sums_a * factor_a + sums_b * factor_b,
        (shaped_a + shaped_b).reshape(mixed_a.shape),
    )


def on_device(
    hidden_in,
    attn_gain,
    w_query,
    w_keyval,
    w_out,
    kv_cache,
    cache_len,
    ffn_gain,
    w_router,
    routes,
    w_gate_up,
    w_down,
    final_gain,
    w_head,
    targets,
):
    seq_count = lax.axis_size("seq")
    seq_index = lax.axis_index("seq")
    col_index = lax.axis_index("col")
    row_index = lax.axis_index("row")
    block_index = lax.axis_index(("seq", "col"))
    own_count = hidden_in.shape[0]
    block_start = seq_index * own_count
    pieces = [hidden_in.reshape(-1), w_query.reshape(-1), w_keyval.reshape(-1), w_out.reshape(-1)]
    bounds = [0]
    for piece in pieces:
        bounds.append(bounds[-1] + piece.shape[0])
    packed = lax.all_gather(jnp.concatenate(pieces), "seq", axis=0, tiled=False)
    shards = packed.shape[0]
    every_row = packed[:, bounds[0] : bounds[1]].reshape((-1,) + hidden_in.shape[1:])
    w_query_all = packed[:, bounds[1] : bounds[2]].reshape((-1,) + w_query.shape[1:])
    w_keyval_all = packed[:, bounds[2] : bounds[3]].reshape((-1,) + w_keyval.shape[1:])
    w_out_all = (
        packed[:, bounds[3] : bounds[4]]
        .reshape((shards,) + w_out.shape)
        .transpose(1, 0, 2)
        .reshape(w_out.shape[0], -1)
    )
    total_rows = every_row.shape[0]
    requests = total_rows // NEW
    width = every_row.shape[1]
    half = width // lax.axis_size("row")
    col_start = row_index * half
    state_in = every_row.astype(jnp.float32)
    normed_in = rms_scale(state_in, attn_gain).astype(jnp.bfloat16)
    query_cols = w_query.shape[1]
    group = query_cols // HD
    query = jnp.dot(
        normed_in,
        w_query_all,
        preferred_element_type=jnp.float32,
    )
    fresh_kv = jnp.dot(
        normed_in,
        w_keyval_all,
        preferred_element_type=jnp.float32,
    )
    fresh_kv = fresh_kv.astype(jnp.bfloat16).reshape(requests, NEW, 2, HD)
    queries = query.reshape(requests, NEW * group, HD)
    scale = HD ** (-0.5)
    length_dev = kv_cache.shape[1]
    cached = kv_cache.reshape(requests, length_dev, 2, HD)
    cached_keys = cached[:, :, 0].astype(jnp.float32)
    cached_values = cached[:, :, 1].astype(jnp.float32)
    old_scores = (
        jnp.einsum("rqd,rpd->rqp", queries, cached_keys, precision=lax.Precision.HIGHEST) * scale
    )
    positions = seq_index * length_dev + jnp.arange(length_dev, dtype=jnp.int32)
    old_mask = (positions[None, :] < cache_len[:, None])[:, None, :]
    fresh_keys = fresh_kv[:, :, 0].astype(jnp.float32)
    fresh_values = fresh_kv[:, :, 1].astype(jnp.float32)
    new_scores = (
        jnp.einsum("rqd,rud->rqu", queries, fresh_keys, precision=lax.Precision.HIGHEST) * scale
    )
    token_of = jnp.arange(NEW * group, dtype=jnp.int32) // group
    new_mask = (
        (token_of[:, None] >= jnp.arange(NEW, dtype=jnp.int32)[None, :]) & (seq_index == 0)
    )[None]
    old_scores = jnp.where(old_mask, old_scores, NEG_LARGE)
    new_scores = jnp.where(new_mask, new_scores, NEG_LARGE)
    highest = jnp.maximum(jnp.max(old_scores, axis=-1), jnp.max(new_scores, axis=-1))
    old_weights = jnp.where(old_mask, jnp.exp(old_scores - highest[..., None]), 0.0)
    new_weights = jnp.where(new_mask, jnp.exp(new_scores - highest[..., None]), 0.0)
    totals = old_weights.sum(-1) + new_weights.sum(-1)
    mixed = jnp.einsum("rqp,rpd->rqd", old_weights, cached_values, precision=lax.Precision.HIGHEST)
    mixed = mixed + jnp.einsum(
        "rqu,rud->rqd", new_weights, fresh_values, precision=lax.Precision.HIGHEST
    )
    highest, totals, mixed = butterfly_merge(
        (highest, totals, mixed.reshape(requests, -1)), "seq", seq_count, merge_softmax
    )
    attended = mixed.reshape(requests, NEW * group, HD) / totals[..., None]
    attn_mix = attended.reshape(total_rows, query_cols).astype(jnp.bfloat16)
    partial_out = jnp.dot(
        attn_mix,
        w_out_all,
        preferred_element_type=jnp.float32,
    )
    state_mid = state_in + lax.psum(partial_out, ("row", "col"))
    own_mid = lax.dynamic_slice_in_dim(state_mid, block_start, own_count, 0)
    normed_mid = rms_scale(state_mid, ffn_gain).astype(jnp.bfloat16)
    router = jnp.dot(normed_mid.astype(jnp.float32), w_router, precision=lax.Precision.HIGHEST)
    chosen = jnp.take_along_axis(router, routes, axis=1)
    probs = jax.nn.sigmoid(chosen - chosen[:, ::-1])
    capacity = 2 * total_rows * TOP // (EXP_DEV * seq_count)
    row_ids = jnp.arange(total_rows, dtype=jnp.int32)
    slot_ids = jnp.arange(capacity, dtype=jnp.int32)
    expert = seq_index * EXP_DEV + 0
    member = routes == expert
    in_row = jnp.any(member, axis=1)
    weight_row = jnp.sum(jnp.where(member, probs, 0.0), axis=1)
    ordering = jnp.cumsum(in_row.astype(jnp.int32)) - 1
    filled = jnp.sum(in_row.astype(jnp.int32))
    source = (
        jnp.zeros((capacity,), jnp.int32)
        .at[jnp.where(in_row, ordering, capacity)]
        .set(row_ids, mode="drop")
    )
    source_list = [source]
    weight_list = [jnp.where(slot_ids < filled, weight_row[source], 0.0)]
    source_all = jnp.stack(source_list)
    weight_all = jnp.stack(weight_list)
    normed_half = lax.dynamic_slice_in_dim(normed_mid, col_start, half, 1)
    expert_rows = normed_half[source_all]
    gate_part = jnp.einsum(
        "ecd,edgf->ecgf", expert_rows, w_gate_up, preferred_element_type=jnp.float32
    )
    gate_both = lax.psum(gate_part, "row")
    expert_hidden = (jax.nn.silu(gate_both[:, :, 0]) * gate_both[:, :, 1]).astype(jnp.bfloat16)
    expert_result = jnp.einsum(
        "ecf,efd->ecd", expert_hidden, w_down, preferred_element_type=jnp.float32
    )
    weighted = (expert_result * weight_all[..., None]).reshape(-1, half)
    term = jnp.zeros((total_rows, half), jnp.float32).at[source_all.reshape(-1)].add(weighted)
    block_count = seq_count * lax.axis_size("col")
    out_count = total_rows // block_count
    block_mid = lax.dynamic_slice_in_dim(
        lax.dynamic_slice_in_dim(state_mid, block_index * out_count, out_count, 0), col_start, half, 1
    )
    state_out = halving_scatter(term, ("seq", "col"), block_count) + block_mid
    layer_out = state_out.astype(jnp.bfloat16)
    gain_half = lax.dynamic_slice_in_dim(final_gain, col_start, half, 0)
    normed_block = final_scale(state_out, gain_half, width)
    normed_out = doubling_gather(normed_block, ("seq", "col"), block_count)
    vocab_dev = w_head.shape[1]
    row_count = total_rows // lax.axis_size("row")
    logits = lax.psum_scatter(
        jnp.dot(normed_out, w_head, preferred_element_type=jnp.float32),
        "row",
        scatter_dimension=0,
        tiled=True,
    )
    own_targets = lax.dynamic_slice_in_dim(targets, row_index * row_count, row_count, 0)
    vocab_start = block_index * vocab_dev
    matches = (
        own_targets[:, None] == (vocab_start + jnp.arange(vocab_dev, dtype=jnp.int32))[None, :]
    )
    picked_local = jnp.sum(jnp.where(matches, logits, 0.0), axis=1)
    local_high = jnp.max(logits, axis=1)
    local_total = jnp.sum(jnp.exp(logits - local_high[:, None]), axis=1)
    row_high, row_total, picked = butterfly_merge(
        (local_high, local_total, picked_local),
        ("seq", "col"),
        seq_count * lax.axis_size("col"),
        merge_logsumexp,
    )
    logprob_part = picked - (row_high + jnp.log(row_total))
    logprob = lax.all_gather(logprob_part, "row", axis=0, tiled=True)
    return (layer_out, logprob)


def solution(mesh):
    return jax.shard_map(
        on_device,
        mesh=mesh,
        in_specs=(
            P("seq", None),
            P(),
            P("seq", ("row", "col")),
            P("seq", ("row", "col")),
            P(("row", "col"), "seq"),
            P(None, "seq", ("row", "col")),
            P(),
            P(),
            P(),
            P(),
            P("seq", "row", None, "col"),
            P("seq", "col", "row"),
            P(),
            P("row", ("seq", "col")),
            P(),
        ),
        out_specs=(P(("seq", "col"), "row"), P()),
        check_vma=False,
    )
```

```python
import jax
import jax.numpy as jnp
from jax import lax
from jax.sharding import PartitionSpec as P

HD = 64
EXP_DEV = 1
TOP = 2
NEW = 4


EPSILON = 1e-05
NEG_LARGE = -1e30


def combined_all(shard, axis, combine):
    everything = jax.tree.map(lambda part: lax.all_gather(part, axis), shard)
    initial = jax.tree.map(lambda part: part[0], everything)

    def lap(k, so_far):
        return combine(so_far, jax.tree.map(lambda part: part[k], everything))

    return lax.fori_loop(1, lax.axis_size(axis), lap, initial)


def butterfly_merge(value, axes, count, combine):
    widths = [part.shape[-1] for part in value]
    edges = [0]
    for width in widths:
        edges.append(edges[-1] + width)

    def split(packed):
        return tuple(packed[..., edges[i] : edges[i + 1]] for i in range(len(widths)))

    packed = jnp.concatenate(value, axis=-1)
    step = 1
    while step < count:
        pairs = [(i, i ^ step) for i in range(count)]
        other = lax.ppermute(packed, axes, pairs)
        packed = jnp.concatenate(combine(split(packed), split(other)), axis=-1)
        step *= 2
    return split(packed)


def halving_scatter(value, axes, count):
    index = lax.axis_index(axes)
    step = count // 2
    while step >= 1:
        half = value.shape[0] // 2
        upper = (index // step) % 2 == 1
        low, high = value[:half], value[half:]
        send = jnp.where(upper, low, high)
        keep = jnp.where(upper, high, low)
        pairs = [(i, i ^ step) for i in range(count)]
        value = keep + lax.ppermute(send, axes, pairs)
        step //= 2
    return value


def doubling_gather(value, axes, count):
    index = lax.axis_index(axes)
    step = 1
    while step < count:
        upper = (index // step) % 2 == 1
        pairs = [(i, i ^ step) for i in range(count)]
        other = lax.ppermute(value, axes, pairs)
        value = jnp.where(
            upper, jnp.concatenate([other, value]), jnp.concatenate([value, other])
        )
        step *= 2
    return value


def merge_logsumexp(first, second):
    high_a, sums_a, picked_a = first
    high_b, sums_b, picked_b = second
    highest = jnp.maximum(high_a, high_b)
    return (
        highest,
        sums_a * jnp.exp(high_a - highest) + sums_b * jnp.exp(high_b - highest),
        picked_a + picked_b,
    )


def rms_scale(values, gain):
    mean_square = jnp.mean(values * values, axis=-1, keepdims=True)
    return values * lax.rsqrt(mean_square + EPSILON) * gain


def final_scale(state, gain_half, width):
    squares = lax.psum(jnp.sum(state * state, axis=-1), "row")
    return (state * lax.rsqrt(squares[:, None] / width + EPSILON) * gain_half).astype(jnp.bfloat16)


def merge_softmax(first, second):
    high_a, sums_a, mixed_a = first
    high_b, sums_b, mixed_b = second
    highest = jnp.maximum(high_a, high_b)
    factor_a = jnp.exp(high_a - highest)
    factor_b = jnp.exp(high_b - highest)
    shaped_a = mixed_a.reshape(highest.shape + (-1,)) * factor_a[..., None]
    shaped_b = mixed_b.reshape(highest.shape + (-1,)) * factor_b[..., None]
    return (
        highest,
        sums_a * factor_a + sums_b * factor_b,
        (shaped_a + shaped_b).reshape(mixed_a.shape),
    )


def on_device(
    hidden_in,
    attn_gain,
    w_query,
    w_keyval,
    w_out,
    kv_cache,
    cache_len,
    ffn_gain,
    w_router,
    routes,
    w_gate_up,
    w_down,
    final_gain,
    w_head,
    targets,
):
    seq_count = lax.axis_size("seq")
    seq_index = lax.axis_index("seq")
    col_index = lax.axis_index("col")
    row_index = lax.axis_index("row")
    block_index = lax.axis_index(("seq", "col"))
    own_count = hidden_in.shape[0]
    block_start = seq_index * own_count
    pieces = [hidden_in.reshape(-1), w_query.reshape(-1), w_keyval.reshape(-1), w_out.reshape(-1)]
    bounds = [0]
    for piece in pieces:
        bounds.append(bounds[-1] + piece.shape[0])
    packed = lax.all_gather(jnp.concatenate(pieces), "seq", axis=0, tiled=False)
    shards = packed.shape[0]
    every_row = packed[:, bounds[0] : bounds[1]].reshape((-1,) + hidden_in.shape[1:])
    w_query_all = packed[:, bounds[1] : bounds[2]].reshape((-1,) + w_query.shape[1:])
    w_keyval_all = packed[:, bounds[2] : bounds[3]].reshape((-1,) + w_keyval.shape[1:])
    w_out_all = (
        packed[:, bounds[3] : bounds[4]]
        .reshape((shards,) + w_out.shape)
        .transpose(1, 0, 2)
        .reshape(w_out.shape[0], -1)
    )
    total_rows = every_row.shape[0]
    requests = total_rows // NEW
    width = every_row.shape[1]
    half = width // lax.axis_size("row")
    col_start = row_index * half
    state_in = every_row.astype(jnp.float32)
    normed_in = rms_scale(state_in, attn_gain).astype(jnp.bfloat16)
    query_cols = w_query.shape[1]
    group = query_cols // HD
    query = jnp.dot(
        normed_in,
        w_query_all,
        preferred_element_type=jnp.float32,
    )
    fresh_kv = jnp.dot(
        normed_in,
        w_keyval_all,
        preferred_element_type=jnp.float32,
    )
    fresh_kv = fresh_kv.astype(jnp.bfloat16).reshape(requests, NEW, 2, HD)
    queries = query.reshape(requests, NEW * group, HD)
    scale = HD ** (-0.5)
    length_dev = kv_cache.shape[1]
    cached = kv_cache.reshape(requests, length_dev, 2, HD)
    cached_keys = cached[:, :, 0].astype(jnp.float32)
    cached_values = cached[:, :, 1].astype(jnp.float32)
    old_scores = (
        jnp.einsum("rqd,rpd->rqp", queries, cached_keys, precision=lax.Precision.HIGHEST) * scale
    )
    positions = seq_index * length_dev + jnp.arange(length_dev, dtype=jnp.int32)
    old_mask = (positions[None, :] < cache_len[:, None])[:, None, :]
    fresh_keys = fresh_kv[:, :, 0].astype(jnp.float32)
    fresh_values = fresh_kv[:, :, 1].astype(jnp.float32)
    new_scores = (
        jnp.einsum("rqd,rud->rqu", queries, fresh_keys, precision=lax.Precision.HIGHEST) * scale
    )
    token_of = jnp.arange(NEW * group, dtype=jnp.int32) // group
    new_mask = (
        (token_of[:, None] >= jnp.arange(NEW, dtype=jnp.int32)[None, :]) & (seq_index == 0)
    )[None]
    old_scores = jnp.where(old_mask, old_scores, NEG_LARGE)
    new_scores = jnp.where(new_mask, new_scores, NEG_LARGE)
    highest = jnp.maximum(jnp.max(old_scores, axis=-1), jnp.max(new_scores, axis=-1))
    old_weights = jnp.where(old_mask, jnp.exp(old_scores - highest[..., None]), 0.0)
    new_weights = jnp.where(new_mask, jnp.exp(new_scores - highest[..., None]), 0.0)
    totals = old_weights.sum(-1) + new_weights.sum(-1)
    mixed = jnp.einsum("rqp,rpd->rqd", old_weights, cached_values, precision=lax.Precision.HIGHEST)
    mixed = mixed + jnp.einsum(
        "rqu,rud->rqd", new_weights, fresh_values, precision=lax.Precision.HIGHEST
    )
    highest, totals, mixed = butterfly_merge(
        (highest, totals, mixed.reshape(requests, -1)), "seq", seq_count, merge_softmax
    )
    attended = mixed.reshape(requests, NEW * group, HD) / totals[..., None]
    attn_mix = attended.reshape(total_rows, query_cols).astype(jnp.bfloat16)
    partial_out = jnp.dot(
        attn_mix,
        w_out_all,
        preferred_element_type=jnp.float32,
    )
    state_mid = state_in + lax.psum(partial_out, ("row", "col"))
    own_mid = lax.dynamic_slice_in_dim(state_mid, block_start, own_count, 0)
    normed_mid = rms_scale(state_mid, ffn_gain).astype(jnp.bfloat16)
    router = jnp.dot(normed_mid.astype(jnp.float32), w_router, precision=lax.Precision.HIGHEST)
    chosen = jnp.take_along_axis(router, routes, axis=1)
    probs = jax.nn.sigmoid(chosen - chosen[:, ::-1])
    capacity = 2 * total_rows * TOP // (EXP_DEV * seq_count)
    row_ids = jnp.arange(total_rows, dtype=jnp.int32)
    slot_ids = jnp.arange(capacity, dtype=jnp.int32)
    expert = seq_index * EXP_DEV + 0
    member = routes == expert
    in_row = jnp.any(member, axis=1)
    weight_row = jnp.sum(jnp.where(member, probs, 0.0), axis=1)
    ordering = jnp.cumsum(in_row.astype(jnp.int32)) - 1
    filled = jnp.sum(in_row.astype(jnp.int32))
    source = (
        jnp.zeros((capacity,), jnp.int32)
        .at[jnp.where(in_row, ordering, capacity)]
        .set(row_ids, mode="drop")
    )
    source_list = [source]
    weight_list = [jnp.where(slot_ids < filled, weight_row[source], 0.0)]
    source_all = jnp.stack(source_list)
    weight_all = jnp.stack(weight_list)
    normed_half = lax.dynamic_slice_in_dim(normed_mid, col_start, half, 1)
    expert_rows = normed_half[source_all]
    gate_part = jnp.einsum(
        "ecd,edgf->ecgf", expert_rows, w_gate_up, preferred_element_type=jnp.float32
    )
    gate_both = lax.psum(gate_part, "row")
    expert_hidden = (jax.nn.silu(gate_both[:, :, 0]) * gate_both[:, :, 1]).astype(jnp.bfloat16)
    expert_result = jnp.einsum(
        "ecf,efd->ecd", expert_hidden, w_down, preferred_element_type=jnp.float32
    )
    weighted = (expert_result * weight_all[..., None]).reshape(-1, half)
    term = jnp.zeros((total_rows, half), jnp.float32).at[source_all.reshape(-1)].add(weighted)
    block_count = seq_count * lax.axis_size("col")
    out_count = total_rows // block_count
    block_mid = lax.dynamic_slice_in_dim(
        lax.dynamic_slice_in_dim(state_mid, block_index * out_count, out_count, 0), col_start, half, 1
    )
    state_out = halving_scatter(term, ("seq", "col"), block_count) + block_mid
    layer_out = state_out.astype(jnp.bfloat16)
    gain_half = lax.dynamic_slice_in_dim(final_gain, col_start, half, 0)
    normed_block = final_scale(state_out, gain_half, width)
    normed_out = doubling_gather(normed_block, ("seq", "col"), block_count)
    vocab_dev = w_head.shape[1]
    row_count = total_rows // lax.axis_size("row")
    logits = lax.psum_scatter(
        jnp.dot(normed_out, w_head, preferred_element_type=jnp.float32),
        "row",
        scatter_dimension=0,
        tiled=True,
    )
    own_targets = lax.dynamic_slice_in_dim(targets, row_index * row_count, row_count, 0)
    vocab_start = block_index * vocab_dev
    matches = (
        own_targets[:, None] == (vocab_start + jnp.arange(vocab_dev, dtype=jnp.int32))[None, :]
    )
    picked_local = jnp.sum(jnp.where(matches, logits, 0.0), axis=1)
    local_high = jnp.max(logits, axis=1)
    local_total = jnp.sum(jnp.exp(logits - local_high[:, None]), axis=1)
    row_high, row_total, picked = butterfly_merge(
        (local_high[None], local_total[None], picked_local[None]),
        ("seq", "col"),
        seq_count * lax.axis_size("col"),
        merge_logsumexp,
    )
    row_high, row_total, picked = row_high[0], row_total[0], picked[0]
    logprob_part = picked - (row_high + jnp.log(row_total))
    logprob = lax.all_gather(logprob_part, "row", axis=0, tiled=True)
    return (layer_out, logprob)


def solution(mesh):
    return jax.shard_map(
        on_device,
        mesh=mesh,
        in_specs=(
            P("seq", None),
            P(),
            P("seq", ("row", "col")),
            P("seq", ("row", "col")),
            P(("row", "col"), "seq"),
            P(None, "seq", ("row", "col")),
            P(),
            P(),
            P(),
            P(),
            P("seq", "row", None, "col"),
            P("seq", "col", "row"),
            P(),
            P("row", ("seq", "col")),
            P(),
        ),
        out_specs=(P(("seq", "col"), "row"), P()),
        check_vma=False,
    )
```

```python
import jax
import jax.numpy as jnp
from jax import lax
from jax.sharding import PartitionSpec as P

HD = 64
EXP_DEV = 1
TOP = 2
NEW = 4


EPSILON = 1e-05
NEG_LARGE = -1e30


def combined_all(shard, axis, combine):
    everything = jax.tree.map(lambda part: lax.all_gather(part, axis), shard)
    initial = jax.tree.map(lambda part: part[0], everything)

    def lap(k, so_far):
        return combine(so_far, jax.tree.map(lambda part: part[k], everything))

    return lax.fori_loop(1, lax.axis_size(axis), lap, initial)


def butterfly_merge(value, axes, count, combine):
    widths = [part.shape[-1] for part in value]
    edges = [0]
    for width in widths:
        edges.append(edges[-1] + width)

    def split(packed):
        return tuple(packed[..., edges[i] : edges[i + 1]] for i in range(len(widths)))

    packed = jnp.concatenate(value, axis=-1)
    step = 1
    while step < count:
        pairs = [(i, i ^ step) for i in range(count)]
        other = lax.ppermute(packed, axes, pairs)
        packed = jnp.concatenate(combine(split(packed), split(other)), axis=-1)
        step *= 2
    return split(packed)


def halving_merge(value, axes, count, combine):
    widths = [part.shape[-1] for part in value]
    edges = [0]
    for width in widths:
        edges.append(edges[-1] + width)

    def split(packed):
        return tuple(packed[..., edges[i] : edges[i + 1]] for i in range(len(widths)))

    index = lax.axis_index(axes)
    packed = jnp.concatenate(value, axis=-1)
    step = count // 2
    while step >= 1:
        half = packed.shape[0] // 2
        upper = (index // step) % 2 == 1
        low, high = packed[:half], packed[half:]
        send = jnp.where(upper, low, high)
        keep = jnp.where(upper, high, low)
        pairs = [(i, i ^ step) for i in range(count)]
        other = lax.ppermute(send, axes, pairs)
        packed = jnp.concatenate(combine(split(keep), split(other)), axis=-1)
        step //= 2
    return split(packed)


def halving_scatter(value, axes, count):
    index = lax.axis_index(axes)
    step = count // 2
    while step >= 1:
        half = value.shape[0] // 2
        upper = (index // step) % 2 == 1
        low, high = value[:half], value[half:]
        send = jnp.where(upper, low, high)
        keep = jnp.where(upper, high, low)
        pairs = [(i, i ^ step) for i in range(count)]
        value = keep + lax.ppermute(send, axes, pairs)
        step //= 2
    return value


def doubling_gather(value, axes, count):
    index = lax.axis_index(axes)
    step = 1
    while step < count:
        upper = (index // step) % 2 == 1
        pairs = [(i, i ^ step) for i in range(count)]
        other = lax.ppermute(value, axes, pairs)
        value = jnp.where(
            upper, jnp.concatenate([other, value]), jnp.concatenate([value, other])
        )
        step *= 2
    return value


def merge_logsumexp(first, second):
    high_a, sums_a, picked_a = first
    high_b, sums_b, picked_b = second
    highest = jnp.maximum(high_a, high_b)
    return (
        highest,
        sums_a * jnp.exp(high_a - highest) + sums_b * jnp.exp(high_b - highest),
        picked_a + picked_b,
    )


def rms_scale(values, gain):
    mean_square = jnp.mean(values * values, axis=-1, keepdims=True)
    return values * lax.rsqrt(mean_square + EPSILON) * gain


def final_scale(state, gain_half, width):
    squares = lax.psum(jnp.sum(state * state, axis=-1), "row")
    return (state * lax.rsqrt(squares[:, None] / width + EPSILON) * gain_half).astype(jnp.bfloat16)


def merge_softmax(first, second):
    high_a, sums_a, mixed_a = first
    high_b, sums_b, mixed_b = second
    highest = jnp.maximum(high_a, high_b)
    factor_a = jnp.exp(high_a - highest)
    factor_b = jnp.exp(high_b - highest)
    shaped_a = mixed_a.reshape(highest.shape + (-1,)) * factor_a[..., None]
    shaped_b = mixed_b.reshape(highest.shape + (-1,)) * factor_b[..., None]
    return (
        highest,
        sums_a * factor_a + sums_b * factor_b,
        (shaped_a + shaped_b).reshape(mixed_a.shape),
    )


def on_device(
    hidden_in,
    attn_gain,
    w_query,
    w_keyval,
    w_out,
    kv_cache,
    cache_len,
    ffn_gain,
    w_router,
    routes,
    w_gate_up,
    w_down,
    final_gain,
    w_head,
    targets,
):
    seq_count = lax.axis_size("seq")
    seq_index = lax.axis_index("seq")
    col_index = lax.axis_index("col")
    row_index = lax.axis_index("row")
    block_index = lax.axis_index(("seq", "col"))
    own_count = hidden_in.shape[0]
    block_start = seq_index * own_count
    pieces = [hidden_in.reshape(-1), w_query.reshape(-1), w_keyval.reshape(-1), w_out.reshape(-1)]
    bounds = [0]
    for piece in pieces:
        bounds.append(bounds[-1] + piece.shape[0])
    packed = lax.all_gather(jnp.concatenate(pieces), "seq", axis=0, tiled=False)
    shards = packed.shape[0]
    every_row = packed[:, bounds[0] : bounds[1]].reshape((-1,) + hidden_in.shape[1:])
    w_query_all = packed[:, bounds[1] : bounds[2]].reshape((-1,) + w_query.shape[1:])
    w_keyval_all = packed[:, bounds[2] : bounds[3]].reshape((-1,) + w_keyval.shape[1:])
    w_out_all = (
        packed[:, bounds[3] : bounds[4]]
        .reshape((shards,) + w_out.shape)
        .transpose(1, 0, 2)
        .reshape(w_out.shape[0], -1)
    )
    total_rows = every_row.shape[0]
    requests = total_rows // NEW
    width = every_row.shape[1]
    half = width // lax.axis_size("row")
    col_start = row_index * half
    state_in = every_row.astype(jnp.float32)
    normed_in = rms_scale(state_in, attn_gain).astype(jnp.bfloat16)
    query_cols = w_query.shape[1]
    group = query_cols // HD
    query = jnp.dot(
        normed_in,
        w_query_all,
        preferred_element_type=jnp.float32,
    )
    fresh_kv = jnp.dot(
        normed_in,
        w_keyval_all,
        preferred_element_type=jnp.float32,
    )
    fresh_kv = fresh_kv.astype(jnp.bfloat16).reshape(requests, NEW, 2, HD)
    queries = query.reshape(requests, NEW * group, HD)
    scale = HD ** (-0.5)
    length_dev = kv_cache.shape[1]
    cached = kv_cache.reshape(requests, length_dev, 2, HD)
    cached_keys = cached[:, :, 0].astype(jnp.float32)
    cached_values = cached[:, :, 1].astype(jnp.float32)
    old_scores = (
        jnp.einsum("rqd,rpd->rqp", queries, cached_keys, precision=lax.Precision.HIGHEST) * scale
    )
    positions = seq_index * length_dev + jnp.arange(length_dev, dtype=jnp.int32)
    old_mask = (positions[None, :] < cache_len[:, None])[:, None, :]
    fresh_keys = fresh_kv[:, :, 0].astype(jnp.float32)
    fresh_values = fresh_kv[:, :, 1].astype(jnp.float32)
    new_scores = (
        jnp.einsum("rqd,rud->rqu", queries, fresh_keys, precision=lax.Precision.HIGHEST) * scale
    )
    token_of = jnp.arange(NEW * group, dtype=jnp.int32) // group
    new_mask = (
        (token_of[:, None] >= jnp.arange(NEW, dtype=jnp.int32)[None, :]) & (seq_index == 0)
    )[None]
    old_scores = jnp.where(old_mask, old_scores, NEG_LARGE)
    new_scores = jnp.where(new_mask, new_scores, NEG_LARGE)
    highest = jnp.maximum(jnp.max(old_scores, axis=-1), jnp.max(new_scores, axis=-1))
    old_weights = jnp.where(old_mask, jnp.exp(old_scores - highest[..., None]), 0.0)
    new_weights = jnp.where(new_mask, jnp.exp(new_scores - highest[..., None]), 0.0)
    totals = old_weights.sum(-1) + new_weights.sum(-1)
    mixed = jnp.einsum("rqp,rpd->rqd", old_weights, cached_values, precision=lax.Precision.HIGHEST)
    mixed = mixed + jnp.einsum(
        "rqu,rud->rqd", new_weights, fresh_values, precision=lax.Precision.HIGHEST
    )
    highest, totals, mixed = halving_merge(
        (highest, totals, mixed.reshape(requests, -1)), "seq", seq_count, merge_softmax
    )
    own_requests = requests // seq_count
    attended = mixed.reshape(own_requests, NEW * group, HD) / totals[..., None]
    attn_mix = attended.reshape(own_count, query_cols).astype(jnp.bfloat16)
    partial_out = jnp.dot(
        attn_mix,
        w_out_all,
        preferred_element_type=jnp.float32,
    )
    own_mid = hidden_in.astype(jnp.float32) + lax.psum(partial_out, ("row", "col"))
    own_normed = rms_scale(own_mid, ffn_gain).astype(jnp.bfloat16)
    normed_mid = doubling_gather(own_normed, "seq", seq_count)
    router = jnp.dot(normed_mid.astype(jnp.float32), w_router, precision=lax.Precision.HIGHEST)
    chosen = jnp.take_along_axis(router, routes, axis=1)
    probs = jax.nn.sigmoid(chosen - chosen[:, ::-1])
    capacity = 2 * total_rows * TOP // (EXP_DEV * seq_count)
    row_ids = jnp.arange(total_rows, dtype=jnp.int32)
    slot_ids = jnp.arange(capacity, dtype=jnp.int32)
    expert = seq_index * EXP_DEV + 0
    member = routes == expert
    in_row = jnp.any(member, axis=1)
    weight_row = jnp.sum(jnp.where(member, probs, 0.0), axis=1)
    ordering = jnp.cumsum(in_row.astype(jnp.int32)) - 1
    filled = jnp.sum(in_row.astype(jnp.int32))
    source = (
        jnp.zeros((capacity,), jnp.int32)
        .at[jnp.where(in_row, ordering, capacity)]
        .set(row_ids, mode="drop")
    )
    source_list = [source]
    weight_list = [jnp.where(slot_ids < filled, weight_row[source], 0.0)]
    source_all = jnp.stack(source_list)
    weight_all = jnp.stack(weight_list)
    normed_half = lax.dynamic_slice_in_dim(normed_mid, col_start, half, 1)
    expert_rows = normed_half[source_all]
    gate_part = jnp.einsum(
        "ecd,edgf->ecgf", expert_rows, w_gate_up, preferred_element_type=jnp.float32
    )
    gate_both = lax.psum(gate_part, "row")
    expert_hidden = (jax.nn.silu(gate_both[:, :, 0]) * gate_both[:, :, 1]).astype(jnp.bfloat16)
    expert_result = jnp.einsum(
        "ecf,efd->ecd", expert_hidden, w_down, preferred_element_type=jnp.float32
    )
    weighted = (expert_result * weight_all[..., None]).reshape(-1, half)
    term = jnp.zeros((total_rows, half), jnp.float32).at[source_all.reshape(-1)].add(weighted)
    block_count = seq_count * lax.axis_size("col")
    out_count = total_rows // block_count
    block_mid = lax.dynamic_slice_in_dim(
        lax.dynamic_slice_in_dim(own_mid, col_index * out_count, out_count, 0), col_start, half, 1
    )
    state_out = halving_scatter(term, ("seq", "col"), block_count) + block_mid
    layer_out = state_out.astype(jnp.bfloat16)
    gain_half = lax.dynamic_slice_in_dim(final_gain, col_start, half, 0)
    normed_block = final_scale(state_out, gain_half, width)
    normed_out = doubling_gather(normed_block, ("seq", "col"), block_count)
    vocab_dev = w_head.shape[1]
    row_count = total_rows // lax.axis_size("row")
    logits = lax.psum_scatter(
        jnp.dot(normed_out, w_head, preferred_element_type=jnp.float32),
        "row",
        scatter_dimension=0,
        tiled=True,
    )
    own_targets = lax.dynamic_slice_in_dim(targets, row_index * row_count, row_count, 0)
    vocab_start = block_index * vocab_dev
    matches = (
        own_targets[:, None] == (vocab_start + jnp.arange(vocab_dev, dtype=jnp.int32))[None, :]
    )
    picked_local = jnp.sum(jnp.where(matches, logits, 0.0), axis=1)
    local_high = jnp.max(logits, axis=1)
    local_total = jnp.sum(jnp.exp(logits - local_high[:, None]), axis=1)
    row_high, row_total, picked = butterfly_merge(
        (local_high[None], local_total[None], picked_local[None]),
        ("seq", "col"),
        seq_count * lax.axis_size("col"),
        merge_logsumexp,
    )
    row_high, row_total, picked = row_high[0], row_total[0], picked[0]
    logprob_part = picked - (row_high + jnp.log(row_total))
    logprob = lax.all_gather(logprob_part, "row", axis=0, tiled=True)
    return (layer_out, logprob)


def solution(mesh):
    return jax.shard_map(
        on_device,
        mesh=mesh,
        in_specs=(
            P("seq", None),
            P(),
            P("seq", ("row", "col")),
            P("seq", ("row", "col")),
            P(("row", "col"), "seq"),
            P(None, "seq", ("row", "col")),
            P(),
            P(),
            P(),
            P(),
            P("seq", "row", None, "col"),
            P("seq", "col", "row"),
            P(),
            P("row", ("seq", "col")),
            P(),
        ),
        out_specs=(P(("seq", "col"), "row"), P()),
        check_vma=False,
    )
```

```python
import jax
import jax.numpy as jnp
from jax import lax
from jax.sharding import PartitionSpec as P

HD = 64
EXP_DEV = 1
TOP = 2
NEW = 4


EPSILON = 1e-05
NEG_LARGE = -1e30


def combined_all(shard, axis, combine):
    everything = jax.tree.map(lambda part: lax.all_gather(part, axis), shard)
    initial = jax.tree.map(lambda part: part[0], everything)

    def lap(k, so_far):
        return combine(so_far, jax.tree.map(lambda part: part[k], everything))

    return lax.fori_loop(1, lax.axis_size(axis), lap, initial)


def butterfly_merge(value, axes, count, combine):
    widths = [part.shape[-1] for part in value]
    edges = [0]
    for width in widths:
        edges.append(edges[-1] + width)

    def split(packed):
        return tuple(packed[..., edges[i] : edges[i + 1]] for i in range(len(widths)))

    packed = jnp.concatenate(value, axis=-1)
    step = 1
    while step < count:
        pairs = [(i, i ^ step) for i in range(count)]
        other = lax.ppermute(packed, axes, pairs)
        packed = jnp.concatenate(combine(split(packed), split(other)), axis=-1)
        step *= 2
    return split(packed)


def halving_merge(value, axes, count, combine):
    widths = [part.shape[-1] for part in value]
    edges = [0]
    for width in widths:
        edges.append(edges[-1] + width)

    def split(packed):
        return tuple(packed[..., edges[i] : edges[i + 1]] for i in range(len(widths)))

    index = lax.axis_index(axes)
    packed = jnp.concatenate(value, axis=-1)
    step = count // 2
    while step >= 1:
        half = packed.shape[0] // 2
        upper = (index // step) % 2 == 1
        low, high = packed[:half], packed[half:]
        send = jnp.where(upper, low, high)
        keep = jnp.where(upper, high, low)
        pairs = [(i, i ^ step) for i in range(count)]
        other = lax.ppermute(send, axes, pairs)
        packed = jnp.concatenate(combine(split(keep), split(other)), axis=-1)
        step //= 2
    return split(packed)


def butterfly_sum(value, axes, count):
    step = 1
    while step < count:
        pairs = [(i, i ^ step) for i in range(count)]
        value = value + lax.ppermute(value, axes, pairs)
        step *= 2
    return value


def halving_scatter(value, axes, count):
    index = lax.axis_index(axes)
    step = count // 2
    while step >= 1:
        half = value.shape[0] // 2
        upper = (index // step) % 2 == 1
        low, high = value[:half], value[half:]
        send = jnp.where(upper, low, high)
        keep = jnp.where(upper, high, low)
        pairs = [(i, i ^ step) for i in range(count)]
        value = keep + lax.ppermute(send, axes, pairs)
        step //= 2
    return value


def doubling_gather(value, axes, count):
    index = lax.axis_index(axes)
    step = 1
    while step < count:
        upper = (index // step) % 2 == 1
        pairs = [(i, i ^ step) for i in range(count)]
        other = lax.ppermute(value, axes, pairs)
        value = jnp.where(
            upper, jnp.concatenate([other, value]), jnp.concatenate([value, other])
        )
        step *= 2
    return value


def merge_logsumexp(first, second):
    high_a, sums_a, picked_a = first
    high_b, sums_b, picked_b = second
    highest = jnp.maximum(high_a, high_b)
    return (
        highest,
        sums_a * jnp.exp(high_a - highest) + sums_b * jnp.exp(high_b - highest),
        picked_a + picked_b,
    )


def rms_scale(values, gain):
    mean_square = jnp.mean(values * values, axis=-1, keepdims=True)
    return values * lax.rsqrt(mean_square + EPSILON) * gain


def final_scale(state, gain_half, width):
    squares = lax.psum(jnp.sum(state * state, axis=-1), "row")
    return (state * lax.rsqrt(squares[:, None] / width + EPSILON) * gain_half).astype(jnp.bfloat16)


def merge_softmax(first, second):
    high_a, sums_a, mixed_a = first
    high_b, sums_b, mixed_b = second
    highest = jnp.maximum(high_a, high_b)
    factor_a = jnp.exp(high_a - highest)
    factor_b = jnp.exp(high_b - highest)
    shaped_a = mixed_a.reshape(highest.shape + (-1,)) * factor_a[..., None]
    shaped_b = mixed_b.reshape(highest.shape + (-1,)) * factor_b[..., None]
    return (
        highest,
        sums_a * factor_a + sums_b * factor_b,
        (shaped_a + shaped_b).reshape(mixed_a.shape),
    )


def on_device(
    hidden_in,
    attn_gain,
    w_query,
    w_keyval,
    w_out,
    kv_cache,
    cache_len,
    ffn_gain,
    w_router,
    routes,
    w_gate_up,
    w_down,
    final_gain,
    w_head,
    targets,
):
    seq_count = lax.axis_size("seq")
    seq_index = lax.axis_index("seq")
    col_index = lax.axis_index("col")
    row_index = lax.axis_index("row")
    block_index = lax.axis_index(("seq", "col"))
    own_count = hidden_in.shape[0]
    block_start = seq_index * own_count
    pieces = [hidden_in.reshape(-1), w_query.reshape(-1), w_keyval.reshape(-1), w_out.reshape(-1)]
    bounds = [0]
    for piece in pieces:
        bounds.append(bounds[-1] + piece.shape[0])
    packed = lax.all_gather(jnp.concatenate(pieces), "seq", axis=0, tiled=False)
    shards = packed.shape[0]
    every_row = packed[:, bounds[0] : bounds[1]].reshape((-1,) + hidden_in.shape[1:])
    w_query_all = packed[:, bounds[1] : bounds[2]].reshape((-1,) + w_query.shape[1:])
    w_keyval_all = packed[:, bounds[2] : bounds[3]].reshape((-1,) + w_keyval.shape[1:])
    w_out_all = (
        packed[:, bounds[3] : bounds[4]]
        .reshape((shards,) + w_out.shape)
        .transpose(1, 0, 2)
        .reshape(w_out.shape[0], -1)
    )
    total_rows = every_row.shape[0]
    requests = total_rows // NEW
    width = every_row.shape[1]
    half = width // lax.axis_size("row")
    col_start = row_index * half
    state_in = every_row.astype(jnp.float32)
    normed_in = rms_scale(state_in, attn_gain).astype(jnp.bfloat16)
    query_cols = w_query.shape[1]
    group = query_cols // HD
    query = jnp.dot(
        normed_in,
        w_query_all,
        preferred_element_type=jnp.float32,
    )
    fresh_kv = jnp.dot(
        normed_in,
        w_keyval_all,
        preferred_element_type=jnp.float32,
    )
    fresh_kv = fresh_kv.astype(jnp.bfloat16).reshape(requests, NEW, 2, HD)
    queries = query.reshape(requests, NEW * group, HD)
    scale = HD ** (-0.5)
    length_dev = kv_cache.shape[1]
    cached = kv_cache.reshape(requests, length_dev, 2, HD)
    cached_keys = cached[:, :, 0].astype(jnp.float32)
    cached_values = cached[:, :, 1].astype(jnp.float32)
    old_scores = (
        jnp.einsum("rqd,rpd->rqp", queries, cached_keys, precision=lax.Precision.HIGHEST) * scale
    )
    positions = seq_index * length_dev + jnp.arange(length_dev, dtype=jnp.int32)
    old_mask = (positions[None, :] < cache_len[:, None])[:, None, :]
    fresh_keys = fresh_kv[:, :, 0].astype(jnp.float32)
    fresh_values = fresh_kv[:, :, 1].astype(jnp.float32)
    new_scores = (
        jnp.einsum("rqd,rud->rqu", queries, fresh_keys, precision=lax.Precision.HIGHEST) * scale
    )
    token_of = jnp.arange(NEW * group, dtype=jnp.int32) // group
    new_mask = (
        (token_of[:, None] >= jnp.arange(NEW, dtype=jnp.int32)[None, :]) & (seq_index == 0)
    )[None]
    old_scores = jnp.where(old_mask, old_scores, NEG_LARGE)
    new_scores = jnp.where(new_mask, new_scores, NEG_LARGE)
    highest = jnp.maximum(jnp.max(old_scores, axis=-1), jnp.max(new_scores, axis=-1))
    old_weights = jnp.where(old_mask, jnp.exp(old_scores - highest[..., None]), 0.0)
    new_weights = jnp.where(new_mask, jnp.exp(new_scores - highest[..., None]), 0.0)
    totals = old_weights.sum(-1) + new_weights.sum(-1)
    mixed = jnp.einsum("rqp,rpd->rqd", old_weights, cached_values, precision=lax.Precision.HIGHEST)
    mixed = mixed + jnp.einsum(
        "rqu,rud->rqd", new_weights, fresh_values, precision=lax.Precision.HIGHEST
    )
    highest, totals, mixed = halving_merge(
        (highest, totals, mixed.reshape(requests, -1)), "seq", seq_count, merge_softmax
    )
    own_requests = requests // seq_count
    attended = mixed.reshape(own_requests, NEW * group, HD) / totals[..., None]
    attn_mix = attended.reshape(own_count, query_cols).astype(jnp.bfloat16)
    partial_out = jnp.dot(
        attn_mix,
        w_out_all,
        preferred_element_type=jnp.float32,
    )
    own_mid = hidden_in.astype(jnp.float32) + butterfly_sum(
        partial_out, ("row", "col"), lax.axis_size("row") * lax.axis_size("col")
    )
    own_normed = rms_scale(own_mid, ffn_gain).astype(jnp.bfloat16)
    normed_mid = doubling_gather(own_normed, "seq", seq_count)
    router = jnp.dot(normed_mid.astype(jnp.float32), w_router, precision=lax.Precision.HIGHEST)
    chosen = jnp.take_along_axis(router, routes, axis=1)
    probs = jax.nn.sigmoid(chosen - chosen[:, ::-1])
    capacity = 2 * total_rows * TOP // (EXP_DEV * seq_count)
    row_ids = jnp.arange(total_rows, dtype=jnp.int32)
    slot_ids = jnp.arange(capacity, dtype=jnp.int32)
    expert = seq_index * EXP_DEV + 0
    member = routes == expert
    in_row = jnp.any(member, axis=1)
    weight_row = jnp.sum(jnp.where(member, probs, 0.0), axis=1)
    ordering = jnp.cumsum(in_row.astype(jnp.int32)) - 1
    filled = jnp.sum(in_row.astype(jnp.int32))
    source = (
        jnp.zeros((capacity,), jnp.int32)
        .at[jnp.where(in_row, ordering, capacity)]
        .set(row_ids, mode="drop")
    )
    source_list = [source]
    weight_list = [jnp.where(slot_ids < filled, weight_row[source], 0.0)]
    source_all = jnp.stack(source_list)
    weight_all = jnp.stack(weight_list)
    normed_half = lax.dynamic_slice_in_dim(normed_mid, col_start, half, 1)
    expert_rows = normed_half[source_all]
    gate_part = jnp.einsum(
        "ecd,edgf->ecgf", expert_rows, w_gate_up, preferred_element_type=jnp.float32
    )
    gate_both = butterfly_sum(gate_part, "row", lax.axis_size("row"))
    expert_hidden = (jax.nn.silu(gate_both[:, :, 0]) * gate_both[:, :, 1]).astype(jnp.bfloat16)
    expert_result = jnp.einsum(
        "ecf,efd->ecd", expert_hidden, w_down, preferred_element_type=jnp.float32
    )
    weighted = (expert_result * weight_all[..., None]).reshape(-1, half)
    term = jnp.zeros((total_rows, half), jnp.float32).at[source_all.reshape(-1)].add(weighted)
    block_count = seq_count * lax.axis_size("col")
    out_count = total_rows // block_count
    block_mid = lax.dynamic_slice_in_dim(
        lax.dynamic_slice_in_dim(own_mid, col_index * out_count, out_count, 0), col_start, half, 1
    )
    state_out = halving_scatter(term, ("seq", "col"), block_count) + block_mid
    layer_out = state_out.astype(jnp.bfloat16)
    gain_half = lax.dynamic_slice_in_dim(final_gain, col_start, half, 0)
    normed_block = final_scale(state_out, gain_half, width)
    normed_out = doubling_gather(normed_block, ("seq", "col"), block_count)
    vocab_dev = w_head.shape[1]
    row_count = total_rows // lax.axis_size("row")
    logits = halving_scatter(
        jnp.dot(normed_out, w_head, preferred_element_type=jnp.float32),
        "row",
        lax.axis_size("row"),
    )
    own_targets = lax.dynamic_slice_in_dim(targets, row_index * row_count, row_count, 0)
    vocab_start = block_index * vocab_dev
    matches = (
        own_targets[:, None] == (vocab_start + jnp.arange(vocab_dev, dtype=jnp.int32))[None, :]
    )
    picked_local = jnp.sum(jnp.where(matches, logits, 0.0), axis=1)
    local_high = jnp.max(logits, axis=1)
    local_total = jnp.sum(jnp.exp(logits - local_high[:, None]), axis=1)
    row_high, row_total, picked = butterfly_merge(
        (local_high[None], local_total[None], picked_local[None]),
        ("seq", "col"),
        seq_count * lax.axis_size("col"),
        merge_logsumexp,
    )
    row_high, row_total, picked = row_high[0], row_total[0], picked[0]
    logprob_part = picked - (row_high + jnp.log(row_total))
    logprob = lax.all_gather(logprob_part, "row", axis=0, tiled=True)
    return (layer_out, logprob)


def solution(mesh):
    return jax.shard_map(
        on_device,
        mesh=mesh,
        in_specs=(
            P("seq", None),
            P(),
            P("seq", ("row", "col")),
            P("seq", ("row", "col")),
            P(("row", "col"), "seq"),
            P(None, "seq", ("row", "col")),
            P(),
            P(),
            P(),
            P(),
            P("seq", "row", None, "col"),
            P("seq", "col", "row"),
            P(),
            P("row", ("seq", "col")),
            P(),
        ),
        out_specs=(P(("seq", "col"), "row"), P()),
        check_vma=False,
    )
```

```python
import jax
import jax.numpy as jnp
from jax import lax
from jax.sharding import PartitionSpec as P

HD = 64
EXP_DEV = 1
TOP = 2
NEW = 4


EPSILON = 1e-05
NEG_LARGE = -1e30


def combined_all(shard, axis, combine):
    everything = jax.tree.map(lambda part: lax.all_gather(part, axis), shard)
    initial = jax.tree.map(lambda part: part[0], everything)

    def lap(k, so_far):
        return combine(so_far, jax.tree.map(lambda part: part[k], everything))

    return lax.fori_loop(1, lax.axis_size(axis), lap, initial)


def radices_of(axes):
    names = (axes,) if isinstance(axes, str) else tuple(axes)
    radices = []
    for name in reversed(names):
        size = lax.axis_size(name)
        while size > 1:
            radix = 4 if size % 4 == 0 else 2
            radices.append(radix)
            size //= radix
    return radices


def group_exchange(value, axes, stride, radix, count, chunks=None):
    digit = (lax.axis_index(axes) // stride) % radix
    received = [value if chunks is None else chunks(digit)]
    for offset in range(1, radix):
        pairs = []
        for i in range(count):
            own = (i // stride) % radix
            pairs.append((i, i + ((own + offset) % radix - own) * stride))
        sent = value if chunks is None else chunks((digit + offset) % radix)
        received.append(lax.ppermute(sent, axes, pairs))
    ordered = []
    for source in range(radix):
        offset = (digit - source) % radix
        picked = received[0]
        for other in range(1, radix):
            picked = jnp.where(offset == other, received[other], picked)
        ordered.append(picked)
    return ordered


def fold(parts, combine):
    while len(parts) > 1:
        parts = [combine(parts[i], parts[i + 1]) for i in range(0, len(parts), 2)]
    return parts[0]


def packer(value):
    edges = [0]
    for part in value:
        edges.append(edges[-1] + part.shape[-1])

    def split(packed):
        return tuple(packed[..., edges[i] : edges[i + 1]] for i in range(len(value)))

    def combine_with(combine):
        return lambda a, b: jnp.concatenate(combine(split(a), split(b)), axis=-1)

    return jnp.concatenate(value, axis=-1), split, combine_with


def butterfly_merge(value, axes, count, combine):
    packed, split, combine_with = packer(value)
    stride = 1
    for radix in radices_of(axes):
        packed = fold(group_exchange(packed, axes, stride, radix, count), combine_with(combine))
        stride *= radix
    return split(packed)


def scatter_steps(packed, axes, count, joined):
    radices = radices_of(axes)
    strides = [1]
    for radix in radices:
        strides.append(strides[-1] * radix)
    for position in reversed(range(len(radices))):
        radix = radices[position]
        size = packed.shape[0] // radix
        whole = packed
        chunks = lambda k, whole=whole, size=size: lax.dynamic_slice_in_dim(whole, k * size, size, 0)
        parts = group_exchange(whole, axes, strides[position], radix, count, chunks)
        packed = fold(parts, joined)
    return packed


def halving_merge(value, axes, count, combine):
    packed, split, combine_with = packer(value)
    return split(scatter_steps(packed, axes, count, combine_with(combine)))


def butterfly_sum(value, axes, count):
    stride = 1
    for radix in radices_of(axes):
        value = fold(group_exchange(value, axes, stride, radix, count), lambda a, b: a + b)
        stride *= radix
    return value


def halving_scatter(value, axes, count):
    return scatter_steps(value, axes, count, lambda a, b: a + b)


def doubling_gather(value, axes, count):
    stride = 1
    for radix in radices_of(axes):
        value = jnp.concatenate(group_exchange(value, axes, stride, radix, count), axis=0)
        stride *= radix
    return value


def merge_logsumexp(first, second):
    high_a, sums_a, picked_a = first
    high_b, sums_b, picked_b = second
    highest = jnp.maximum(high_a, high_b)
    return (
        highest,
        sums_a * jnp.exp(high_a - highest) + sums_b * jnp.exp(high_b - highest),
        picked_a + picked_b,
    )


def rms_scale(values, gain):
    mean_square = jnp.mean(values * values, axis=-1, keepdims=True)
    return values * lax.rsqrt(mean_square + EPSILON) * gain


def final_scale(state, gain_half, width):
    squares = lax.psum(jnp.sum(state * state, axis=-1), "row")
    return (state * lax.rsqrt(squares[:, None] / width + EPSILON) * gain_half).astype(jnp.bfloat16)


def merge_softmax(first, second):
    high_a, sums_a, mixed_a = first
    high_b, sums_b, mixed_b = second
    highest = jnp.maximum(high_a, high_b)
    factor_a = jnp.exp(high_a - highest)
    factor_b = jnp.exp(high_b - highest)
    shaped_a = mixed_a.reshape(highest.shape + (-1,)) * factor_a[..., None]
    shaped_b = mixed_b.reshape(highest.shape + (-1,)) * factor_b[..., None]
    return (
        highest,
        sums_a * factor_a + sums_b * factor_b,
        (shaped_a + shaped_b).reshape(mixed_a.shape),
    )


def on_device(
    hidden_in,
    attn_gain,
    w_query,
    w_keyval,
    w_out,
    kv_cache,
    cache_len,
    ffn_gain,
    w_router,
    routes,
    w_gate_up,
    w_down,
    final_gain,
    w_head,
    targets,
):
    seq_count = lax.axis_size("seq")
    seq_index = lax.axis_index("seq")
    col_index = lax.axis_index("col")
    row_index = lax.axis_index("row")
    block_index = lax.axis_index(("seq", "col"))
    own_count = hidden_in.shape[0]
    block_start = seq_index * own_count
    pieces = [hidden_in.reshape(-1), w_query.reshape(-1), w_keyval.reshape(-1), w_out.reshape(-1)]
    bounds = [0]
    for piece in pieces:
        bounds.append(bounds[-1] + piece.shape[0])
    packed = lax.all_gather(jnp.concatenate(pieces), "seq", axis=0, tiled=False)
    shards = packed.shape[0]
    every_row = packed[:, bounds[0] : bounds[1]].reshape((-1,) + hidden_in.shape[1:])
    w_query_all = packed[:, bounds[1] : bounds[2]].reshape((-1,) + w_query.shape[1:])
    w_keyval_all = packed[:, bounds[2] : bounds[3]].reshape((-1,) + w_keyval.shape[1:])
    w_out_all = (
        packed[:, bounds[3] : bounds[4]]
        .reshape((shards,) + w_out.shape)
        .transpose(1, 0, 2)
        .reshape(w_out.shape[0], -1)
    )
    total_rows = every_row.shape[0]
    requests = total_rows // NEW
    width = every_row.shape[1]
    half = width // lax.axis_size("row")
    col_start = row_index * half
    state_in = every_row.astype(jnp.float32)
    normed_in = rms_scale(state_in, attn_gain).astype(jnp.bfloat16)
    query_cols = w_query.shape[1]
    group = query_cols // HD
    query = jnp.dot(
        normed_in,
        w_query_all,
        preferred_element_type=jnp.float32,
    )
    fresh_kv = jnp.dot(
        normed_in,
        w_keyval_all,
        preferred_element_type=jnp.float32,
    )
    fresh_kv = fresh_kv.astype(jnp.bfloat16).reshape(requests, NEW, 2, HD)
    queries = query.reshape(requests, NEW * group, HD)
    scale = HD ** (-0.5)
    length_dev = kv_cache.shape[1]
    cached = kv_cache.reshape(requests, length_dev, 2, HD)
    cached_keys = cached[:, :, 0].astype(jnp.float32)
    cached_values = cached[:, :, 1].astype(jnp.float32)
    old_scores = (
        jnp.einsum("rqd,rpd->rqp", queries, cached_keys, precision=lax.Precision.HIGHEST) * scale
    )
    positions = seq_index * length_dev + jnp.arange(length_dev, dtype=jnp.int32)
    old_mask = (positions[None, :] < cache_len[:, None])[:, None, :]
    fresh_keys = fresh_kv[:, :, 0].astype(jnp.float32)
    fresh_values = fresh_kv[:, :, 1].astype(jnp.float32)
    new_scores = (
        jnp.einsum("rqd,rud->rqu", queries, fresh_keys, precision=lax.Precision.HIGHEST) * scale
    )
    token_of = jnp.arange(NEW * group, dtype=jnp.int32) // group
    new_mask = (
        (token_of[:, None] >= jnp.arange(NEW, dtype=jnp.int32)[None, :]) & (seq_index == 0)
    )[None]
    old_scores = jnp.where(old_mask, old_scores, NEG_LARGE)
    new_scores = jnp.where(new_mask, new_scores, NEG_LARGE)
    highest = jnp.maximum(jnp.max(old_scores, axis=-1), jnp.max(new_scores, axis=-1))
    old_weights = jnp.where(old_mask, jnp.exp(old_scores - highest[..., None]), 0.0)
    new_weights = jnp.where(new_mask, jnp.exp(new_scores - highest[..., None]), 0.0)
    totals = old_weights.sum(-1) + new_weights.sum(-1)
    mixed = jnp.einsum("rqp,rpd->rqd", old_weights, cached_values, precision=lax.Precision.HIGHEST)
    mixed = mixed + jnp.einsum(
        "rqu,rud->rqd", new_weights, fresh_values, precision=lax.Precision.HIGHEST
    )
    highest, totals, mixed = halving_merge(
        (highest, totals, mixed.reshape(requests, -1)), "seq", seq_count, merge_softmax
    )
    own_requests = requests // seq_count
    attended = mixed.reshape(own_requests, NEW * group, HD) / totals[..., None]
    attn_mix = attended.reshape(own_count, query_cols).astype(jnp.bfloat16)
    partial_out = jnp.dot(
        attn_mix,
        w_out_all,
        preferred_element_type=jnp.float32,
    )
    own_mid = hidden_in.astype(jnp.float32) + butterfly_sum(
        partial_out, ("row", "col"), lax.axis_size("row") * lax.axis_size("col")
    )
    own_normed = rms_scale(own_mid, ffn_gain).astype(jnp.bfloat16)
    normed_mid = doubling_gather(own_normed, "seq", seq_count)
    router = jnp.dot(normed_mid.astype(jnp.float32), w_router, precision=lax.Precision.HIGHEST)
    chosen = jnp.take_along_axis(router, routes, axis=1)
    probs = jax.nn.sigmoid(chosen - chosen[:, ::-1])
    capacity = 2 * total_rows * TOP // (EXP_DEV * seq_count)
    row_ids = jnp.arange(total_rows, dtype=jnp.int32)
    slot_ids = jnp.arange(capacity, dtype=jnp.int32)
    expert = seq_index * EXP_DEV + 0
    member = routes == expert
    in_row = jnp.any(member, axis=1)
    weight_row = jnp.sum(jnp.where(member, probs, 0.0), axis=1)
    ordering = jnp.cumsum(in_row.astype(jnp.int32)) - 1
    filled = jnp.sum(in_row.astype(jnp.int32))
    source = (
        jnp.zeros((capacity,), jnp.int32)
        .at[jnp.where(in_row, ordering, capacity)]
        .set(row_ids, mode="drop")
    )
    source_list = [source]
    weight_list = [jnp.where(slot_ids < filled, weight_row[source], 0.0)]
    source_all = jnp.stack(source_list)
    weight_all = jnp.stack(weight_list)
    normed_half = lax.dynamic_slice_in_dim(normed_mid, col_start, half, 1)
    expert_rows = normed_half[source_all]
    gate_part = jnp.einsum(
        "ecd,edgf->ecgf", expert_rows, w_gate_up, preferred_element_type=jnp.float32
    )
    gate_both = butterfly_sum(gate_part, "row", lax.axis_size("row"))
    expert_hidden = (jax.nn.silu(gate_both[:, :, 0]) * gate_both[:, :, 1]).astype(jnp.bfloat16)
    expert_result = jnp.einsum(
        "ecf,efd->ecd", expert_hidden, w_down, preferred_element_type=jnp.float32
    )
    weighted = (expert_result * weight_all[..., None]).reshape(-1, half)
    term = jnp.zeros((total_rows, half), jnp.float32).at[source_all.reshape(-1)].add(weighted)
    block_count = seq_count * lax.axis_size("col")
    out_count = total_rows // block_count
    block_mid = lax.dynamic_slice_in_dim(
        lax.dynamic_slice_in_dim(own_mid, col_index * out_count, out_count, 0), col_start, half, 1
    )
    state_out = halving_scatter(term, ("seq", "col"), block_count) + block_mid
    layer_out = state_out.astype(jnp.bfloat16)
    gain_half = lax.dynamic_slice_in_dim(final_gain, col_start, half, 0)
    normed_block = final_scale(state_out, gain_half, width)
    normed_out = doubling_gather(normed_block, ("seq", "col"), block_count)
    vocab_dev = w_head.shape[1]
    row_count = total_rows // lax.axis_size("row")
    logits = halving_scatter(
        jnp.dot(normed_out, w_head, preferred_element_type=jnp.float32),
        "row",
        lax.axis_size("row"),
    )
    own_targets = lax.dynamic_slice_in_dim(targets, row_index * row_count, row_count, 0)
    vocab_start = block_index * vocab_dev
    matches = (
        own_targets[:, None] == (vocab_start + jnp.arange(vocab_dev, dtype=jnp.int32))[None, :]
    )
    picked_local = jnp.sum(jnp.where(matches, logits, 0.0), axis=1)
    local_high = jnp.max(logits, axis=1)
    local_total = jnp.sum(jnp.exp(logits - local_high[:, None]), axis=1)
    row_high, row_total, picked = butterfly_merge(
        (local_high[None], local_total[None], picked_local[None]),
        ("seq", "col"),
        seq_count * lax.axis_size("col"),
        merge_logsumexp,
    )
    row_high, row_total, picked = row_high[0], row_total[0], picked[0]
    logprob_part = picked - (row_high + jnp.log(row_total))
    logprob = lax.all_gather(logprob_part, "row", axis=0, tiled=True)
    return (layer_out, logprob)


def solution(mesh):
    return jax.shard_map(
        on_device,
        mesh=mesh,
        in_specs=(
            P("seq", None),
            P(),
            P("seq", ("row", "col")),
            P("seq", ("row", "col")),
            P(("row", "col"), "seq"),
            P(None, "seq", ("row", "col")),
            P(),
            P(),
            P(),
            P(),
            P("seq", "row", None, "col"),
            P("seq", "col", "row"),
            P(),
            P("row", ("seq", "col")),
            P(),
        ),
        out_specs=(P(("seq", "col"), "row"), P()),
        check_vma=False,
    )
```

```python
import jax
import jax.numpy as jnp
from jax import lax
from jax.sharding import PartitionSpec as P
from jax.experimental import pallas as pl
from jax.experimental.pallas import tpu as pltpu

HD = 64
EXP_DEV = 1
TOP = 2
NEW = 4


EPSILON = 1e-05
NEG_LARGE = -1e30


def combined_all(shard, axis, combine):
    everything = jax.tree.map(lambda part: lax.all_gather(part, axis), shard)
    initial = jax.tree.map(lambda part: part[0], everything)

    def lap(k, so_far):
        return combine(so_far, jax.tree.map(lambda part: part[k], everything))

    return lax.fori_loop(1, lax.axis_size(axis), lap, initial)


def radices_of(axes):
    names = (axes,) if isinstance(axes, str) else tuple(axes)
    radices = []
    for name in reversed(names):
        size = lax.axis_size(name)
        while size > 1:
            radix = 4 if size % 4 == 0 else 2
            radices.append(radix)
            size //= radix
    return radices


def group_exchange(value, axes, stride, radix, count, chunks=None):
    digit = (lax.axis_index(axes) // stride) % radix
    received = [value if chunks is None else chunks(digit)]
    for offset in range(1, radix):
        pairs = []
        for i in range(count):
            own = (i // stride) % radix
            pairs.append((i, i + ((own + offset) % radix - own) * stride))
        sent = value if chunks is None else chunks((digit + offset) % radix)
        received.append(lax.ppermute(sent, axes, pairs))
    ordered = []
    for source in range(radix):
        offset = (digit - source) % radix
        picked = received[0]
        for other in range(1, radix):
            picked = jnp.where(offset == other, received[other], picked)
        ordered.append(picked)
    return ordered


def fold(parts, combine):
    while len(parts) > 1:
        parts = [combine(parts[i], parts[i + 1]) for i in range(0, len(parts), 2)]
    return parts[0]


def packer(value):
    edges = [0]
    for part in value:
        edges.append(edges[-1] + part.shape[-1])

    def split(packed):
        return tuple(packed[..., edges[i] : edges[i + 1]] for i in range(len(value)))

    def combine_with(combine):
        return lambda a, b: jnp.concatenate(combine(split(a), split(b)), axis=-1)

    return jnp.concatenate(value, axis=-1), split, combine_with


def butterfly_merge(value, axes, count, combine):
    packed, split, combine_with = packer(value)
    stride = 1
    for radix in radices_of(axes):
        packed = fold(group_exchange(packed, axes, stride, radix, count), combine_with(combine))
        stride *= radix
    return split(packed)


def scatter_steps(packed, axes, count, joined):
    radices = radices_of(axes)
    strides = [1]
    for radix in radices:
        strides.append(strides[-1] * radix)
    for position in reversed(range(len(radices))):
        radix = radices[position]
        size = packed.shape[0] // radix
        whole = packed
        chunks = lambda k, whole=whole, size=size: lax.dynamic_slice_in_dim(whole, k * size, size, 0)
        parts = group_exchange(whole, axes, strides[position], radix, count, chunks)
        packed = fold(parts, joined)
    return packed


def halving_merge(value, axes, count, combine):
    packed, split, combine_with = packer(value)
    return split(scatter_steps(packed, axes, count, combine_with(combine)))


def butterfly_sum(value, axes, count):
    stride = 1
    for radix in radices_of(axes):
        value = fold(group_exchange(value, axes, stride, radix, count), lambda a, b: a + b)
        stride *= radix
    return value


def halving_scatter(value, axes, count):
    return scatter_steps(value, axes, count, lambda a, b: a + b)


def doubling_gather(value, axes, count):
    stride = 1
    for radix in radices_of(axes):
        value = jnp.concatenate(group_exchange(value, axes, stride, radix, count), axis=0)
        stride *= radix
    return value


def merge_logsumexp(first, second):
    high_a, sums_a, picked_a = first
    high_b, sums_b, picked_b = second
    highest = jnp.maximum(high_a, high_b)
    return (
        highest,
        sums_a * jnp.exp(high_a - highest) + sums_b * jnp.exp(high_b - highest),
        picked_a + picked_b,
    )


ATTN_BLOCK = 4


def cached_attention_kernel(lens_ref, q_ref, kv_ref, out_ref):
    first = pl.program_id(0) * ATTN_BLOCK
    contract_last = (((1,), (1,)), ((), ()))
    for i in range(ATTN_BLOCK):
        length = lens_ref[first + i]
        q = q_ref[i]
        kv = kv_ref[i]
        q_hi = q.astype(jnp.bfloat16)
        q_lo = (q - q_hi.astype(jnp.float32)).astype(jnp.bfloat16)
        s = lax.dot_general(q_hi, kv, contract_last, preferred_element_type=jnp.float32)
        s = s + lax.dot_general(q_lo, kv, contract_last, preferred_element_type=jnp.float32)
        s = s * (HD ** (-0.5))
        mask = lax.broadcasted_iota(jnp.int32, s.shape, 1) < length
        s = jnp.where(mask, s, NEG_LARGE)
        high = jnp.max(s, axis=1, keepdims=True)
        p = jnp.where(mask, jnp.exp(s - high), 0.0)
        total = jnp.sum(p, axis=1, keepdims=True)
        p_hi = p.astype(jnp.bfloat16)
        p_lo = (p - p_hi.astype(jnp.float32)).astype(jnp.bfloat16)
        acc = jnp.dot(p_hi, kv, preferred_element_type=jnp.float32)
        acc = acc + jnp.dot(p_lo, kv, preferred_element_type=jnp.float32)
        col = lax.broadcasted_iota(jnp.int32, acc.shape, 1)
        out_ref[i] = jnp.where(col == 0, high, jnp.where(col == 1, total, acc))


def cached_attention(local_lens, q_padded, kv):
    requests, rows, lanes = q_padded.shape
    length = kv.shape[1]
    grid_spec = pltpu.PrefetchScalarGridSpec(
        num_scalar_prefetch=1,
        grid=(requests // ATTN_BLOCK,),
        in_specs=[
            pl.BlockSpec((ATTN_BLOCK, rows, lanes), lambda r, lens: (r, 0, 0)),
            pl.BlockSpec((ATTN_BLOCK, length, lanes), lambda r, lens: (r, 0, 0)),
        ],
        out_specs=pl.BlockSpec((ATTN_BLOCK, rows, lanes), lambda r, lens: (r, 0, 0)),
    )
    return pl.pallas_call(
        cached_attention_kernel,
        grid_spec=grid_spec,
        out_shape=jax.ShapeDtypeStruct((requests, rows, lanes), jnp.float32),
    )(local_lens, q_padded, kv)


def rms_scale(values, gain):
    mean_square = jnp.mean(values * values, axis=-1, keepdims=True)
    return values * lax.rsqrt(mean_square + EPSILON) * gain


def final_scale(state, gain_half, width):
    squares = lax.psum(jnp.sum(state * state, axis=-1), "row")
    return (state * lax.rsqrt(squares[:, None] / width + EPSILON) * gain_half).astype(jnp.bfloat16)


def merge_softmax(first, second):
    high_a, sums_a, mixed_a = first
    high_b, sums_b, mixed_b = second
    highest = jnp.maximum(high_a, high_b)
    factor_a = jnp.exp(high_a - highest)
    factor_b = jnp.exp(high_b - highest)
    shaped_a = mixed_a.reshape(highest.shape + (-1,)) * factor_a[..., None]
    shaped_b = mixed_b.reshape(highest.shape + (-1,)) * factor_b[..., None]
    return (
        highest,
        sums_a * factor_a + sums_b * factor_b,
        (shaped_a + shaped_b).reshape(mixed_a.shape),
    )


def on_device(
    hidden_in,
    attn_gain,
    w_query,
    w_keyval,
    w_out,
    kv_cache,
    cache_len,
    ffn_gain,
    w_router,
    routes,
    w_gate_up,
    w_down,
    final_gain,
    w_head,
    targets,
):
    seq_count = lax.axis_size("seq")
    seq_index = lax.axis_index("seq")
    col_index = lax.axis_index("col")
    row_index = lax.axis_index("row")
    block_index = lax.axis_index(("seq", "col"))
    own_count = hidden_in.shape[0]
    block_start = seq_index * own_count
    pieces = [hidden_in.reshape(-1), w_query.reshape(-1), w_keyval.reshape(-1), w_out.reshape(-1)]
    bounds = [0]
    for piece in pieces:
        bounds.append(bounds[-1] + piece.shape[0])
    packed = doubling_gather(jnp.concatenate(pieces)[None], "seq", lax.axis_size("seq"))
    shards = packed.shape[0]
    every_row = packed[:, bounds[0] : bounds[1]].reshape((-1,) + hidden_in.shape[1:])
    w_query_all = packed[:, bounds[1] : bounds[2]].reshape((-1,) + w_query.shape[1:])
    w_keyval_all = packed[:, bounds[2] : bounds[3]].reshape((-1,) + w_keyval.shape[1:])
    w_out_all = (
        packed[:, bounds[3] : bounds[4]]
        .reshape((shards,) + w_out.shape)
        .transpose(1, 0, 2)
        .reshape(w_out.shape[0], -1)
    )
    total_rows = every_row.shape[0]
    requests = total_rows // NEW
    width = every_row.shape[1]
    half = width // lax.axis_size("row")
    col_start = row_index * half
    state_in = every_row.astype(jnp.float32)
    normed_in = rms_scale(state_in, attn_gain).astype(jnp.bfloat16)
    query_cols = w_query.shape[1]
    group = query_cols // HD
    query = jnp.dot(
        normed_in,
        w_query_all,
        preferred_element_type=jnp.float32,
    )
    fresh_kv = jnp.dot(
        normed_in,
        w_keyval_all,
        preferred_element_type=jnp.float32,
    )
    fresh_kv = fresh_kv.astype(jnp.bfloat16).reshape(requests, NEW, 2, HD)
    queries = query.reshape(requests, NEW * group, HD)
    scale = HD ** (-0.5)
    length_dev = kv_cache.shape[1]
    local_lens = jnp.clip(cache_len - seq_index * length_dev, 0, length_dev).astype(jnp.int32)
    q_padded = jnp.concatenate([queries, jnp.zeros_like(queries)], axis=-1)
    cached_out = cached_attention(local_lens, q_padded, kv_cache)
    old_high = cached_out[:, :, 0]
    old_total = cached_out[:, :, 1]
    old_mixed = cached_out[:, :, HD:]
    fresh_keys = fresh_kv[:, :, 0].astype(jnp.float32)
    fresh_values = fresh_kv[:, :, 1].astype(jnp.float32)
    new_scores = (
        jnp.einsum("rqd,rud->rqu", queries, fresh_keys, precision=lax.Precision.HIGHEST) * scale
    )
    token_of = jnp.arange(NEW * group, dtype=jnp.int32) // group
    new_mask = (
        (token_of[:, None] >= jnp.arange(NEW, dtype=jnp.int32)[None, :]) & (seq_index == 0)
    )[None]
    new_scores = jnp.where(new_mask, new_scores, NEG_LARGE)
    new_high = jnp.max(new_scores, axis=-1)
    new_weights = jnp.where(new_mask, jnp.exp(new_scores - new_high[..., None]), 0.0)
    new_mixed = jnp.einsum(
        "rqu,rud->rqd", new_weights, fresh_values, precision=lax.Precision.HIGHEST
    )
    highest, totals, mixed = merge_softmax(
        (old_high, old_total, old_mixed.reshape(requests, -1)),
        (new_high, new_weights.sum(-1), new_mixed.reshape(requests, -1)),
    )
    highest, totals, mixed = halving_merge((highest, totals, mixed), "seq", seq_count, merge_softmax)
    own_requests = requests // seq_count
    attended = mixed.reshape(own_requests, NEW * group, HD) / totals[..., None]
    attn_mix = attended.reshape(own_count, query_cols).astype(jnp.bfloat16)
    partial_out = jnp.dot(
        attn_mix,
        w_out_all,
        preferred_element_type=jnp.float32,
    )
    own_mid = hidden_in.astype(jnp.float32) + butterfly_sum(
        partial_out, ("row", "col"), lax.axis_size("row") * lax.axis_size("col")
    )
    own_normed = rms_scale(own_mid, ffn_gain).astype(jnp.bfloat16)
    normed_mid = doubling_gather(own_normed, "seq", seq_count)
    router = jnp.dot(normed_mid.astype(jnp.float32), w_router, precision=lax.Precision.HIGHEST)
    chosen = jnp.take_along_axis(router, routes, axis=1)
    probs = jax.nn.sigmoid(chosen - chosen[:, ::-1])
    capacity = 2 * total_rows * TOP // (EXP_DEV * seq_count)
    row_ids = jnp.arange(total_rows, dtype=jnp.int32)
    slot_ids = jnp.arange(capacity, dtype=jnp.int32)
    expert = seq_index * EXP_DEV + 0
    member = routes == expert
    in_row = jnp.any(member, axis=1)
    weight_row = jnp.sum(jnp.where(member, probs, 0.0), axis=1)
    ordering = jnp.cumsum(in_row.astype(jnp.int32)) - 1
    filled = jnp.sum(in_row.astype(jnp.int32))
    source = (
        jnp.zeros((capacity,), jnp.int32)
        .at[jnp.where(in_row, ordering, capacity)]
        .set(row_ids, mode="drop")
    )
    source_list = [source]
    weight_list = [jnp.where(slot_ids < filled, weight_row[source], 0.0)]
    source_all = jnp.stack(source_list)
    weight_all = jnp.stack(weight_list)
    normed_half = lax.dynamic_slice_in_dim(normed_mid, col_start, half, 1)
    expert_rows = normed_half[source_all]
    gate_part = jnp.einsum(
        "ecd,edgf->ecgf", expert_rows, w_gate_up, preferred_element_type=jnp.float32
    )
    gate_both = butterfly_sum(gate_part, "row", lax.axis_size("row"))
    expert_hidden = (jax.nn.silu(gate_both[:, :, 0]) * gate_both[:, :, 1]).astype(jnp.bfloat16)
    expert_result = jnp.einsum(
        "ecf,efd->ecd", expert_hidden, w_down, preferred_element_type=jnp.float32
    )
    weighted = (expert_result * weight_all[..., None]).reshape(-1, half)
    term = jnp.zeros((total_rows, half), jnp.float32).at[source_all.reshape(-1)].add(weighted)
    block_count = seq_count * lax.axis_size("col")
    out_count = total_rows // block_count
    block_mid = lax.dynamic_slice_in_dim(
        lax.dynamic_slice_in_dim(own_mid, col_index * out_count, out_count, 0), col_start, half, 1
    )
    state_out = halving_scatter(term, ("seq", "col"), block_count) + block_mid
    layer_out = state_out.astype(jnp.bfloat16)
    gain_half = lax.dynamic_slice_in_dim(final_gain, col_start, half, 0)
    normed_block = final_scale(state_out, gain_half, width)
    normed_out = doubling_gather(normed_block, ("seq", "col"), block_count)
    vocab_dev = w_head.shape[1]
    row_count = total_rows // lax.axis_size("row")
    logits = halving_scatter(
        jnp.dot(normed_out, w_head, preferred_element_type=jnp.float32),
        "row",
        lax.axis_size("row"),
    )
    own_targets = lax.dynamic_slice_in_dim(targets, row_index * row_count, row_count, 0)
    vocab_start = block_index * vocab_dev
    matches = (
        own_targets[:, None] == (vocab_start + jnp.arange(vocab_dev, dtype=jnp.int32))[None, :]
    )
    picked_local = jnp.sum(jnp.where(matches, logits, 0.0), axis=1)
    local_high = jnp.max(logits, axis=1)
    local_total = jnp.sum(jnp.exp(logits - local_high[:, None]), axis=1)
    row_high, row_total, picked = butterfly_merge(
        (local_high[None], local_total[None], picked_local[None]),
        ("seq", "col"),
        seq_count * lax.axis_size("col"),
        merge_logsumexp,
    )
    row_high, row_total, picked = row_high[0], row_total[0], picked[0]
    logprob_part = picked - (row_high + jnp.log(row_total))
    logprob = lax.all_gather(logprob_part, "row", axis=0, tiled=True)
    return (layer_out, logprob)


def solution(mesh):
    return jax.shard_map(
        on_device,
        mesh=mesh,
        in_specs=(
            P("seq", None),
            P(),
            P("seq", ("row", "col")),
            P("seq", ("row", "col")),
            P(("row", "col"), "seq"),
            P(None, "seq", ("row", "col")),
            P(),
            P(),
            P(),
            P(),
            P("seq", "row", None, "col"),
            P("seq", "col", "row"),
            P(),
            P("row", ("seq", "col")),
            P(),
        ),
        out_specs=(P(("seq", "col"), "row"), P()),
        check_vma=False,
    )
```

```python
import jax
import jax.numpy as jnp
from jax import lax
from jax.sharding import PartitionSpec as P

HD = 64
EXP_DEV = 1
TOP = 2
NEW = 4


EPSILON = 1e-05
NEG_LARGE = -1e30


def combined_all(shard, axis, combine):
    everything = jax.tree.map(lambda part: lax.all_gather(part, axis), shard)
    initial = jax.tree.map(lambda part: part[0], everything)

    def lap(k, so_far):
        return combine(so_far, jax.tree.map(lambda part: part[k], everything))

    return lax.fori_loop(1, lax.axis_size(axis), lap, initial)


def radices_of(axes):
    names = (axes,) if isinstance(axes, str) else tuple(axes)
    radices = []
    for name in reversed(names):
        size = lax.axis_size(name)
        while size > 1:
            radix = 4 if size % 4 == 0 else 2
            radices.append(radix)
            size //= radix
    return radices


def group_exchange(value, axes, stride, radix, count, chunks=None):
    digit = (lax.axis_index(axes) // stride) % radix
    received = [value if chunks is None else chunks(digit)]
    for offset in range(1, radix):
        pairs = []
        for i in range(count):
            own = (i // stride) % radix
            pairs.append((i, i + ((own + offset) % radix - own) * stride))
        sent = value if chunks is None else chunks((digit + offset) % radix)
        received.append(lax.ppermute(sent, axes, pairs))
    ordered = []
    for source in range(radix):
        offset = (digit - source) % radix
        picked = received[0]
        for other in range(1, radix):
            picked = jnp.where(offset == other, received[other], picked)
        ordered.append(picked)
    return ordered


def fold(parts, combine):
    while len(parts) > 1:
        parts = [combine(parts[i], parts[i + 1]) for i in range(0, len(parts), 2)]
    return parts[0]


def packer(value):
    edges = [0]
    for part in value:
        edges.append(edges[-1] + part.shape[-1])

    def split(packed):
        return tuple(packed[..., edges[i] : edges[i + 1]] for i in range(len(value)))

    def combine_with(combine):
        return lambda a, b: jnp.concatenate(combine(split(a), split(b)), axis=-1)

    return jnp.concatenate(value, axis=-1), split, combine_with


def butterfly_merge(value, axes, count, combine):
    packed, split, combine_with = packer(value)
    stride = 1
    for radix in radices_of(axes):
        packed = fold(group_exchange(packed, axes, stride, radix, count), combine_with(combine))
        stride *= radix
    return split(packed)


def scatter_steps(packed, axes, count, joined):
    radices = radices_of(axes)
    strides = [1]
    for radix in radices:
        strides.append(strides[-1] * radix)
    for position in reversed(range(len(radices))):
        radix = radices[position]
        size = packed.shape[0] // radix
        whole = packed
        chunks = lambda k, whole=whole, size=size: lax.dynamic_slice_in_dim(whole, k * size, size, 0)
        parts = group_exchange(whole, axes, strides[position], radix, count, chunks)
        packed = fold(parts, joined)
    return packed


def halving_merge(value, axes, count, combine):
    packed, split, combine_with = packer(value)
    return split(scatter_steps(packed, axes, count, combine_with(combine)))


def butterfly_sum(value, axes, count):
    stride = 1
    for radix in radices_of(axes):
        value = fold(group_exchange(value, axes, stride, radix, count), lambda a, b: a + b)
        stride *= radix
    return value


def halving_scatter(value, axes, count):
    return scatter_steps(value, axes, count, lambda a, b: a + b)


def doubling_gather(value, axes, count):
    stride = 1
    for radix in radices_of(axes):
        value = jnp.concatenate(group_exchange(value, axes, stride, radix, count), axis=0)
        stride *= radix
    return value


def merge_logsumexp(first, second):
    high_a, sums_a, picked_a = first
    high_b, sums_b, picked_b = second
    highest = jnp.maximum(high_a, high_b)
    return (
        highest,
        sums_a * jnp.exp(high_a - highest) + sums_b * jnp.exp(high_b - highest),
        picked_a + picked_b,
    )


def rms_scale(values, gain):
    mean_square = jnp.mean(values * values, axis=-1, keepdims=True)
    return values * lax.rsqrt(mean_square + EPSILON) * gain


def final_scale(state, gain_half, width):
    squares = lax.psum(jnp.sum(state * state, axis=-1), "row")
    return (state * lax.rsqrt(squares[:, None] / width + EPSILON) * gain_half).astype(jnp.bfloat16)


def merge_softmax(first, second):
    high_a, sums_a, mixed_a = first
    high_b, sums_b, mixed_b = second
    highest = jnp.maximum(high_a, high_b)
    factor_a = jnp.exp(high_a - highest)
    factor_b = jnp.exp(high_b - highest)
    shaped_a = mixed_a.reshape(highest.shape + (-1,)) * factor_a[..., None]
    shaped_b = mixed_b.reshape(highest.shape + (-1,)) * factor_b[..., None]
    return (
        highest,
        sums_a * factor_a + sums_b * factor_b,
        (shaped_a + shaped_b).reshape(mixed_a.shape),
    )


def on_device(
    hidden_in,
    attn_gain,
    w_query,
    w_keyval,
    w_out,
    kv_cache,
    cache_len,
    ffn_gain,
    w_router,
    routes,
    w_gate_up,
    w_down,
    final_gain,
    w_head,
    targets,
):
    seq_count = lax.axis_size("seq")
    seq_index = lax.axis_index("seq")
    col_index = lax.axis_index("col")
    row_index = lax.axis_index("row")
    block_index = lax.axis_index(("seq", "col"))
    own_count = hidden_in.shape[0]
    block_start = seq_index * own_count
    pieces = [hidden_in.reshape(-1), w_query.reshape(-1), w_keyval.reshape(-1)]
    bounds = [0]
    for piece in pieces:
        bounds.append(bounds[-1] + piece.shape[0])
    packed = lax.all_gather(jnp.concatenate(pieces), "seq", axis=0, tiled=False)
    shards = packed.shape[0]
    every_row = packed[:, bounds[0] : bounds[1]].reshape((-1,) + hidden_in.shape[1:])
    w_query_all = packed[:, bounds[1] : bounds[2]].reshape((-1,) + w_query.shape[1:])
    w_keyval_all = packed[:, bounds[2] : bounds[3]].reshape((-1,) + w_keyval.shape[1:])
    w_out_all = (
        doubling_gather(w_out[None], "seq", lax.axis_size("seq"))
        .transpose(1, 0, 2)
        .reshape(w_out.shape[0], -1)
    )
    total_rows = every_row.shape[0]
    requests = total_rows // NEW
    width = every_row.shape[1]
    half = width // lax.axis_size("row")
    col_start = row_index * half
    state_in = every_row.astype(jnp.float32)
    normed_in = rms_scale(state_in, attn_gain).astype(jnp.bfloat16)
    query_cols = w_query.shape[1]
    group = query_cols // HD
    query = jnp.dot(
        normed_in,
        w_query_all,
        preferred_element_type=jnp.float32,
    )
    fresh_kv = jnp.dot(
        normed_in,
        w_keyval_all,
        preferred_element_type=jnp.float32,
    )
    fresh_kv = fresh_kv.astype(jnp.bfloat16).reshape(requests, NEW, 2, HD)
    queries = query.reshape(requests, NEW * group, HD)
    scale = HD ** (-0.5)
    length_dev = kv_cache.shape[1]
    cached = kv_cache.reshape(requests, length_dev, 2, HD)
    cached_keys = cached[:, :, 0].astype(jnp.float32)
    cached_values = cached[:, :, 1].astype(jnp.float32)
    old_scores = (
        jnp.einsum("rqd,rpd->rqp", queries, cached_keys, precision=lax.Precision.HIGHEST) * scale
    )
    positions = seq_index * length_dev + jnp.arange(length_dev, dtype=jnp.int32)
    old_mask = (positions[None, :] < cache_len[:, None])[:, None, :]
    fresh_keys = fresh_kv[:, :, 0].astype(jnp.float32)
    fresh_values = fresh_kv[:, :, 1].astype(jnp.float32)
    new_scores = (
        jnp.einsum("rqd,rud->rqu", queries, fresh_keys, precision=lax.Precision.HIGHEST) * scale
    )
    token_of = jnp.arange(NEW * group, dtype=jnp.int32) // group
    new_mask = (
        (token_of[:, None] >= jnp.arange(NEW, dtype=jnp.int32)[None, :]) & (seq_index == 0)
    )[None]
    old_scores = jnp.where(old_mask, old_scores, NEG_LARGE)
    new_scores = jnp.where(new_mask, new_scores, NEG_LARGE)
    highest = jnp.maximum(jnp.max(old_scores, axis=-1), jnp.max(new_scores, axis=-1))
    old_weights = jnp.where(old_mask, jnp.exp(old_scores - highest[..., None]), 0.0)
    new_weights = jnp.where(new_mask, jnp.exp(new_scores - highest[..., None]), 0.0)
    totals = old_weights.sum(-1) + new_weights.sum(-1)
    mixed = jnp.einsum("rqp,rpd->rqd", old_weights, cached_values, precision=lax.Precision.HIGHEST)
    mixed = mixed + jnp.einsum(
        "rqu,rud->rqd", new_weights, fresh_values, precision=lax.Precision.HIGHEST
    )
    highest, totals, mixed = halving_merge(
        (highest, totals, mixed.reshape(requests, -1)), "seq", seq_count, merge_softmax
    )
    own_requests = requests // seq_count
    attended = mixed.reshape(own_requests, NEW * group, HD) / totals[..., None]
    attn_mix = attended.reshape(own_count, query_cols).astype(jnp.bfloat16)
    partial_out = jnp.dot(
        attn_mix,
        w_out_all,
        preferred_element_type=jnp.float32,
    )
    own_mid = hidden_in.astype(jnp.float32) + butterfly_sum(
        partial_out, ("row", "col"), lax.axis_size("row") * lax.axis_size("col")
    )
    own_normed = rms_scale(own_mid, ffn_gain).astype(jnp.bfloat16)
    normed_mid = doubling_gather(own_normed, "seq", seq_count)
    router = jnp.dot(normed_mid.astype(jnp.float32), w_router, precision=lax.Precision.HIGHEST)
    chosen = jnp.take_along_axis(router, routes, axis=1)
    probs = jax.nn.sigmoid(chosen - chosen[:, ::-1])
    capacity = 2 * total_rows * TOP // (EXP_DEV * seq_count)
    row_ids = jnp.arange(total_rows, dtype=jnp.int32)
    slot_ids = jnp.arange(capacity, dtype=jnp.int32)
    expert = seq_index * EXP_DEV + 0
    member = routes == expert
    in_row = jnp.any(member, axis=1)
    weight_row = jnp.sum(jnp.where(member, probs, 0.0), axis=1)
    ordering = jnp.cumsum(in_row.astype(jnp.int32)) - 1
    filled = jnp.sum(in_row.astype(jnp.int32))
    source = (
        jnp.zeros((capacity,), jnp.int32)
        .at[jnp.where(in_row, ordering, capacity)]
        .set(row_ids, mode="drop")
    )
    source_list = [source]
    weight_list = [jnp.where(slot_ids < filled, weight_row[source], 0.0)]
    source_all = jnp.stack(source_list)
    weight_all = jnp.stack(weight_list)
    normed_half = lax.dynamic_slice_in_dim(normed_mid, col_start, half, 1)
    expert_rows = normed_half[source_all]
    gate_part = jnp.einsum(
        "ecd,edgf->ecgf", expert_rows, w_gate_up, preferred_element_type=jnp.float32
    )
    gate_both = butterfly_sum(gate_part, "row", lax.axis_size("row"))
    expert_hidden = (jax.nn.silu(gate_both[:, :, 0]) * gate_both[:, :, 1]).astype(jnp.bfloat16)
    expert_result = jnp.einsum(
        "ecf,efd->ecd", expert_hidden, w_down, preferred_element_type=jnp.float32
    )
    weighted = (expert_result * weight_all[..., None]).reshape(-1, half)
    term = jnp.zeros((total_rows, half), jnp.float32).at[source_all.reshape(-1)].add(weighted)
    block_count = seq_count * lax.axis_size("col")
    out_count = total_rows // block_count
    block_mid = lax.dynamic_slice_in_dim(
        lax.dynamic_slice_in_dim(own_mid, col_index * out_count, out_count, 0), col_start, half, 1
    )
    state_out = halving_scatter(term, ("seq", "col"), block_count) + block_mid
    layer_out = state_out.astype(jnp.bfloat16)
    gain_half = lax.dynamic_slice_in_dim(final_gain, col_start, half, 0)
    normed_block = final_scale(state_out, gain_half, width)
    normed_out = doubling_gather(normed_block, ("seq", "col"), block_count)
    vocab_dev = w_head.shape[1]
    row_count = total_rows // lax.axis_size("row")
    logits = halving_scatter(
        jnp.dot(normed_out, w_head, preferred_element_type=jnp.float32),
        "row",
        lax.axis_size("row"),
    )
    own_targets = lax.dynamic_slice_in_dim(targets, row_index * row_count, row_count, 0)
    vocab_start = block_index * vocab_dev
    matches = (
        own_targets[:, None] == (vocab_start + jnp.arange(vocab_dev, dtype=jnp.int32))[None, :]
    )
    picked_local = jnp.sum(jnp.where(matches, logits, 0.0), axis=1)
    local_high = jnp.max(logits, axis=1)
    local_total = jnp.sum(jnp.exp(logits - local_high[:, None]), axis=1)
    row_high, row_total, picked = butterfly_merge(
        (local_high[None], local_total[None], picked_local[None]),
        ("seq", "col"),
        seq_count * lax.axis_size("col"),
        merge_logsumexp,
    )
    row_high, row_total, picked = row_high[0], row_total[0], picked[0]
    logprob_part = picked - (row_high + jnp.log(row_total))
    logprob = lax.all_gather(logprob_part, "row", axis=0, tiled=True)
    return (layer_out, logprob)


def solution(mesh):
    return jax.shard_map(
        on_device,
        mesh=mesh,
        in_specs=(
            P("seq", None),
            P(),
            P("seq", ("row", "col")),
            P("seq", ("row", "col")),
            P(("row", "col"), "seq"),
            P(None, "seq", ("row", "col")),
            P(),
            P(),
            P(),
            P(),
            P("seq", "row", None, "col"),
            P("seq", "col", "row"),
            P(),
            P("row", ("seq", "col")),
            P(),
        ),
        out_specs=(P(("seq", "col"), "row"), P()),
        check_vma=False,
    )
```

```python
import jax
import jax.numpy as jnp
from jax import lax
from jax.sharding import PartitionSpec as P

HD = 64
EXP_DEV = 1
TOP = 2
NEW = 4


EPSILON = 1e-05
NEG_LARGE = -1e30


def combined_all(shard, axis, combine):
    everything = jax.tree.map(lambda part: lax.all_gather(part, axis), shard)
    initial = jax.tree.map(lambda part: part[0], everything)

    def lap(k, so_far):
        return combine(so_far, jax.tree.map(lambda part: part[k], everything))

    return lax.fori_loop(1, lax.axis_size(axis), lap, initial)


def radices_of(axes):
    names = (axes,) if isinstance(axes, str) else tuple(axes)
    radices = []
    for name in reversed(names):
        size = lax.axis_size(name)
        while size > 1:
            radix = 4 if size % 4 == 0 else 2
            radices.append(radix)
            size //= radix
    return radices


def group_exchange(value, axes, stride, radix, count, chunks=None):
    digit = (lax.axis_index(axes) // stride) % radix
    received = [value if chunks is None else chunks(digit)]
    for offset in range(1, radix):
        pairs = []
        for i in range(count):
            own = (i // stride) % radix
            pairs.append((i, i + ((own + offset) % radix - own) * stride))
        sent = value if chunks is None else chunks((digit + offset) % radix)
        received.append(lax.ppermute(sent, axes, pairs))
    ordered = []
    for source in range(radix):
        offset = (digit - source) % radix
        picked = received[0]
        for other in range(1, radix):
            picked = jnp.where(offset == other, received[other], picked)
        ordered.append(picked)
    return ordered


def fold(parts, combine):
    while len(parts) > 1:
        parts = [combine(parts[i], parts[i + 1]) for i in range(0, len(parts), 2)]
    return parts[0]


def packer(value):
    edges = [0]
    for part in value:
        edges.append(edges[-1] + part.shape[-1])

    def split(packed):
        return tuple(packed[..., edges[i] : edges[i + 1]] for i in range(len(value)))

    def combine_with(combine):
        return lambda a, b: jnp.concatenate(combine(split(a), split(b)), axis=-1)

    return jnp.concatenate(value, axis=-1), split, combine_with


def butterfly_merge(value, axes, count, combine):
    packed, split, combine_with = packer(value)
    stride = 1
    for radix in radices_of(axes):
        packed = fold(group_exchange(packed, axes, stride, radix, count), combine_with(combine))
        stride *= radix
    return split(packed)


def scatter_steps(packed, axes, count, joined):
    radices = radices_of(axes)
    strides = [1]
    for radix in radices:
        strides.append(strides[-1] * radix)
    for position in reversed(range(len(radices))):
        radix = radices[position]
        size = packed.shape[0] // radix
        whole = packed
        chunks = lambda k, whole=whole, size=size: lax.dynamic_slice_in_dim(whole, k * size, size, 0)
        parts = group_exchange(whole, axes, strides[position], radix, count, chunks)
        packed = fold(parts, joined)
    return packed


def halving_merge(value, axes, count, combine):
    packed, split, combine_with = packer(value)
    return split(scatter_steps(packed, axes, count, combine_with(combine)))


def butterfly_sum(value, axes, count):
    stride = 1
    for radix in radices_of(axes):
        value = fold(group_exchange(value, axes, stride, radix, count), lambda a, b: a + b)
        stride *= radix
    return value


def halving_scatter(value, axes, count):
    return scatter_steps(value, axes, count, lambda a, b: a + b)


def doubling_gather(value, axes, count):
    stride = 1
    for radix in radices_of(axes):
        value = jnp.concatenate(group_exchange(value, axes, stride, radix, count), axis=0)
        stride *= radix
    return value


def merge_logsumexp(first, second):
    high_a, sums_a, picked_a = first
    high_b, sums_b, picked_b = second
    highest = jnp.maximum(high_a, high_b)
    return (
        highest,
        sums_a * jnp.exp(high_a - highest) + sums_b * jnp.exp(high_b - highest),
        picked_a + picked_b,
    )


def rms_scale(values, gain):
    mean_square = jnp.mean(values * values, axis=-1, keepdims=True)
    return values * lax.rsqrt(mean_square + EPSILON) * gain


def final_scale(state, gain_half, width):
    squares = lax.psum(jnp.sum(state * state, axis=-1), "row")
    return (state * lax.rsqrt(squares[:, None] / width + EPSILON) * gain_half).astype(jnp.bfloat16)


def merge_softmax(first, second):
    high_a, sums_a, mixed_a = first
    high_b, sums_b, mixed_b = second
    highest = jnp.maximum(high_a, high_b)
    factor_a = jnp.exp(high_a - highest)
    factor_b = jnp.exp(high_b - highest)
    shaped_a = mixed_a.reshape(highest.shape + (-1,)) * factor_a[..., None]
    shaped_b = mixed_b.reshape(highest.shape + (-1,)) * factor_b[..., None]
    return (
        highest,
        sums_a * factor_a + sums_b * factor_b,
        (shaped_a + shaped_b).reshape(mixed_a.shape),
    )


def on_device(
    hidden_in,
    attn_gain,
    w_query,
    w_keyval,
    w_out,
    kv_cache,
    cache_len,
    ffn_gain,
    w_router,
    routes,
    w_gate_up,
    w_down,
    final_gain,
    w_head,
    targets,
):
    seq_count = lax.axis_size("seq")
    seq_index = lax.axis_index("seq")
    col_index = lax.axis_index("col")
    row_index = lax.axis_index("row")
    block_index = lax.axis_index(("seq", "col"))
    own_count = hidden_in.shape[0]
    block_start = seq_index * own_count
    pieces = [hidden_in.reshape(-1), w_query.reshape(-1), w_keyval.reshape(-1)]
    bounds = [0]
    for piece in pieces:
        bounds.append(bounds[-1] + piece.shape[0])
    packed = lax.all_gather(jnp.concatenate(pieces), "seq", axis=0, tiled=False)
    shards = packed.shape[0]
    every_row = packed[:, bounds[0] : bounds[1]].reshape((-1,) + hidden_in.shape[1:])
    w_query_all = packed[:, bounds[1] : bounds[2]].reshape((-1,) + w_query.shape[1:])
    w_keyval_all = packed[:, bounds[2] : bounds[3]].reshape((-1,) + w_keyval.shape[1:])
    w_out_all = (
        doubling_gather(lax.optimization_barrier((packed, w_out))[1][None], "seq", lax.axis_size("seq"))
        .transpose(1, 0, 2)
        .reshape(w_out.shape[0], -1)
    )
    total_rows = every_row.shape[0]
    requests = total_rows // NEW
    width = every_row.shape[1]
    half = width // lax.axis_size("row")
    col_start = row_index * half
    state_in = every_row.astype(jnp.float32)
    normed_in = rms_scale(state_in, attn_gain).astype(jnp.bfloat16)
    query_cols = w_query.shape[1]
    group = query_cols // HD
    query = jnp.dot(
        normed_in,
        w_query_all,
        preferred_element_type=jnp.float32,
    )
    fresh_kv = jnp.dot(
        normed_in,
        w_keyval_all,
        preferred_element_type=jnp.float32,
    )
    fresh_kv = fresh_kv.astype(jnp.bfloat16).reshape(requests, NEW, 2, HD)
    queries = query.reshape(requests, NEW * group, HD)
    scale = HD ** (-0.5)
    length_dev = kv_cache.shape[1]
    cached = kv_cache.reshape(requests, length_dev, 2, HD)
    cached_keys = cached[:, :, 0].astype(jnp.float32)
    cached_values = cached[:, :, 1].astype(jnp.float32)
    old_scores = (
        jnp.einsum("rqd,rpd->rqp", queries, cached_keys, precision=lax.Precision.HIGHEST) * scale
    )
    positions = seq_index * length_dev + jnp.arange(length_dev, dtype=jnp.int32)
    old_mask = (positions[None, :] < cache_len[:, None])[:, None, :]
    fresh_keys = fresh_kv[:, :, 0].astype(jnp.float32)
    fresh_values = fresh_kv[:, :, 1].astype(jnp.float32)
    new_scores = (
        jnp.einsum("rqd,rud->rqu", queries, fresh_keys, precision=lax.Precision.HIGHEST) * scale
    )
    token_of = jnp.arange(NEW * group, dtype=jnp.int32) // group
    new_mask = (
        (token_of[:, None] >= jnp.arange(NEW, dtype=jnp.int32)[None, :]) & (seq_index == 0)
    )[None]
    old_scores = jnp.where(old_mask, old_scores, NEG_LARGE)
    new_scores = jnp.where(new_mask, new_scores, NEG_LARGE)
    highest = jnp.maximum(jnp.max(old_scores, axis=-1), jnp.max(new_scores, axis=-1))
    old_weights = jnp.where(old_mask, jnp.exp(old_scores - highest[..., None]), 0.0)
    new_weights = jnp.where(new_mask, jnp.exp(new_scores - highest[..., None]), 0.0)
    totals = old_weights.sum(-1) + new_weights.sum(-1)
    mixed = jnp.einsum("rqp,rpd->rqd", old_weights, cached_values, precision=lax.Precision.HIGHEST)
    mixed = mixed + jnp.einsum(
        "rqu,rud->rqd", new_weights, fresh_values, precision=lax.Precision.HIGHEST
    )
    highest, totals, mixed = halving_merge(
        (highest, totals, mixed.reshape(requests, -1)), "seq", seq_count, merge_softmax
    )
    own_requests = requests // seq_count
    attended = mixed.reshape(own_requests, NEW * group, HD) / totals[..., None]
    attn_mix = attended.reshape(own_count, query_cols).astype(jnp.bfloat16)
    partial_out = jnp.dot(
        attn_mix,
        w_out_all,
        preferred_element_type=jnp.float32,
    )
    own_mid = hidden_in.astype(jnp.float32) + butterfly_sum(
        partial_out, ("row", "col"), lax.axis_size("row") * lax.axis_size("col")
    )
    own_normed = rms_scale(own_mid, ffn_gain).astype(jnp.bfloat16)
    normed_mid = doubling_gather(own_normed, "seq", seq_count)
    router = jnp.dot(normed_mid.astype(jnp.float32), w_router, precision=lax.Precision.HIGHEST)
    chosen = jnp.take_along_axis(router, routes, axis=1)
    probs = jax.nn.sigmoid(chosen - chosen[:, ::-1])
    capacity = 2 * total_rows * TOP // (EXP_DEV * seq_count)
    row_ids = jnp.arange(total_rows, dtype=jnp.int32)
    slot_ids = jnp.arange(capacity, dtype=jnp.int32)
    expert = seq_index * EXP_DEV + 0
    member = routes == expert
    in_row = jnp.any(member, axis=1)
    weight_row = jnp.sum(jnp.where(member, probs, 0.0), axis=1)
    ordering = jnp.cumsum(in_row.astype(jnp.int32)) - 1
    filled = jnp.sum(in_row.astype(jnp.int32))
    source = (
        jnp.zeros((capacity,), jnp.int32)
        .at[jnp.where(in_row, ordering, capacity)]
        .set(row_ids, mode="drop")
    )
    source_list = [source]
    weight_list = [jnp.where(slot_ids < filled, weight_row[source], 0.0)]
    source_all = jnp.stack(source_list)
    weight_all = jnp.stack(weight_list)
    normed_half = lax.dynamic_slice_in_dim(normed_mid, col_start, half, 1)
    expert_rows = normed_half[source_all]
    gate_part = jnp.einsum(
        "ecd,edgf->ecgf", expert_rows, w_gate_up, preferred_element_type=jnp.float32
    )
    gate_both = butterfly_sum(gate_part, "row", lax.axis_size("row"))
    expert_hidden = (jax.nn.silu(gate_both[:, :, 0]) * gate_both[:, :, 1]).astype(jnp.bfloat16)
    expert_result = jnp.einsum(
        "ecf,efd->ecd", expert_hidden, w_down, preferred_element_type=jnp.float32
    )
    weighted = (expert_result * weight_all[..., None]).reshape(-1, half)
    term = jnp.zeros((total_rows, half), jnp.float32).at[source_all.reshape(-1)].add(weighted)
    block_count = seq_count * lax.axis_size("col")
    out_count = total_rows // block_count
    block_mid = lax.dynamic_slice_in_dim(
        lax.dynamic_slice_in_dim(own_mid, col_index * out_count, out_count, 0), col_start, half, 1
    )
    state_out = halving_scatter(term, ("seq", "col"), block_count) + block_mid
    layer_out = state_out.astype(jnp.bfloat16)
    gain_half = lax.dynamic_slice_in_dim(final_gain, col_start, half, 0)
    normed_block = final_scale(state_out, gain_half, width)
    normed_out = doubling_gather(normed_block, ("seq", "col"), block_count)
    vocab_dev = w_head.shape[1]
    row_count = total_rows // lax.axis_size("row")
    logits = halving_scatter(
        jnp.dot(normed_out, w_head, preferred_element_type=jnp.float32),
        "row",
        lax.axis_size("row"),
    )
    own_targets = lax.dynamic_slice_in_dim(targets, row_index * row_count, row_count, 0)
    vocab_start = block_index * vocab_dev
    matches = (
        own_targets[:, None] == (vocab_start + jnp.arange(vocab_dev, dtype=jnp.int32))[None, :]
    )
    picked_local = jnp.sum(jnp.where(matches, logits, 0.0), axis=1)
    local_high = jnp.max(logits, axis=1)
    local_total = jnp.sum(jnp.exp(logits - local_high[:, None]), axis=1)
    row_high, row_total, picked = butterfly_merge(
        (local_high[None], local_total[None], picked_local[None]),
        ("seq", "col"),
        seq_count * lax.axis_size("col"),
        merge_logsumexp,
    )
    row_high, row_total, picked = row_high[0], row_total[0], picked[0]
    logprob_part = picked - (row_high + jnp.log(row_total))
    logprob = lax.all_gather(logprob_part, "row", axis=0, tiled=True)
    return (layer_out, logprob)


def solution(mesh):
    return jax.shard_map(
        on_device,
        mesh=mesh,
        in_specs=(
            P("seq", None),
            P(),
            P("seq", ("row", "col")),
            P("seq", ("row", "col")),
            P(("row", "col"), "seq"),
            P(None, "seq", ("row", "col")),
            P(),
            P(),
            P(),
            P(),
            P("seq", "row", None, "col"),
            P("seq", "col", "row"),
            P(),
            P("row", ("seq", "col")),
            P(),
        ),
        out_specs=(P(("seq", "col"), "row"), P()),
        check_vma=False,
    )
```

```python
import jax
import jax.numpy as jnp
from jax import lax
from jax.sharding import PartitionSpec as P

HD = 64
EXP_DEV = 1
TOP = 2
NEW = 4


EPSILON = 1e-05
NEG_LARGE = -1e30


def combined_all(shard, axis, combine):
    everything = jax.tree.map(lambda part: lax.all_gather(part, axis), shard)
    initial = jax.tree.map(lambda part: part[0], everything)

    def lap(k, so_far):
        return combine(so_far, jax.tree.map(lambda part: part[k], everything))

    return lax.fori_loop(1, lax.axis_size(axis), lap, initial)


def radices_of(axes):
    names = (axes,) if isinstance(axes, str) else tuple(axes)
    radices = []
    for name in reversed(names):
        size = lax.axis_size(name)
        while size > 1:
            radix = 4 if size % 4 == 0 else 2
            radices.append(radix)
            size //= radix
    return radices


def group_exchange(value, axes, stride, radix, count, chunks=None):
    digit = (lax.axis_index(axes) // stride) % radix
    received = [value if chunks is None else chunks(digit)]
    for offset in range(1, radix):
        pairs = []
        for i in range(count):
            own = (i // stride) % radix
            pairs.append((i, i + ((own + offset) % radix - own) * stride))
        sent = value if chunks is None else chunks((digit + offset) % radix)
        received.append(lax.ppermute(sent, axes, pairs))
    ordered = []
    for source in range(radix):
        offset = (digit - source) % radix
        picked = received[0]
        for other in range(1, radix):
            picked = jnp.where(offset == other, received[other], picked)
        ordered.append(picked)
    return ordered


def fold(parts, combine):
    while len(parts) > 1:
        parts = [combine(parts[i], parts[i + 1]) for i in range(0, len(parts), 2)]
    return parts[0]


def packer(value):
    edges = [0]
    for part in value:
        edges.append(edges[-1] + part.shape[-1])

    def split(packed):
        return tuple(packed[..., edges[i] : edges[i + 1]] for i in range(len(value)))

    def combine_with(combine):
        return lambda a, b: jnp.concatenate(combine(split(a), split(b)), axis=-1)

    return jnp.concatenate(value, axis=-1), split, combine_with


def butterfly_merge(value, axes, count, combine):
    packed, split, combine_with = packer(value)
    stride = 1
    for radix in radices_of(axes):
        packed = fold(group_exchange(packed, axes, stride, radix, count), combine_with(combine))
        stride *= radix
    return split(packed)


def scatter_steps(packed, axes, count, joined):
    radices = radices_of(axes)
    strides = [1]
    for radix in radices:
        strides.append(strides[-1] * radix)
    for position in reversed(range(len(radices))):
        radix = radices[position]
        size = packed.shape[0] // radix
        whole = packed
        chunks = lambda k, whole=whole, size=size: lax.dynamic_slice_in_dim(whole, k * size, size, 0)
        parts = group_exchange(whole, axes, strides[position], radix, count, chunks)
        packed = fold(parts, joined)
    return packed


def halving_merge(value, axes, count, combine):
    packed, split, combine_with = packer(value)
    return split(scatter_steps(packed, axes, count, combine_with(combine)))


def butterfly_sum(value, axes, count):
    stride = 1
    for radix in radices_of(axes):
        value = fold(group_exchange(value, axes, stride, radix, count), lambda a, b: a + b)
        stride *= radix
    return value


def halving_scatter(value, axes, count):
    return scatter_steps(value, axes, count, lambda a, b: a + b)


def doubling_gather(value, axes, count):
    stride = 1
    for radix in radices_of(axes):
        value = jnp.concatenate(group_exchange(value, axes, stride, radix, count), axis=0)
        stride *= radix
    return value


def merge_logsumexp(first, second):
    high_a, sums_a, picked_a = first
    high_b, sums_b, picked_b = second
    highest = jnp.maximum(high_a, high_b)
    return (
        highest,
        sums_a * jnp.exp(high_a - highest) + sums_b * jnp.exp(high_b - highest),
        picked_a + picked_b,
    )


def rms_scale(values, gain):
    mean_square = jnp.mean(values * values, axis=-1, keepdims=True)
    return values * lax.rsqrt(mean_square + EPSILON) * gain


def final_scale(state, gain_half, width):
    squares = lax.psum(jnp.sum(state * state, axis=-1), "row")
    return (state * lax.rsqrt(squares[:, None] / width + EPSILON) * gain_half).astype(jnp.bfloat16)


def merge_softmax(first, second):
    high_a, sums_a, mixed_a = first
    high_b, sums_b, mixed_b = second
    highest = jnp.maximum(high_a, high_b)
    factor_a = jnp.exp(high_a - highest)
    factor_b = jnp.exp(high_b - highest)
    shaped_a = mixed_a.reshape(highest.shape + (-1,)) * factor_a[..., None]
    shaped_b = mixed_b.reshape(highest.shape + (-1,)) * factor_b[..., None]
    return (
        highest,
        sums_a * factor_a + sums_b * factor_b,
        (shaped_a + shaped_b).reshape(mixed_a.shape),
    )


def on_device(
    hidden_in,
    attn_gain,
    w_query,
    w_keyval,
    w_out,
    kv_cache,
    cache_len,
    ffn_gain,
    w_router,
    routes,
    w_gate_up,
    w_down,
    final_gain,
    w_head,
    targets,
):
    seq_count = lax.axis_size("seq")
    seq_index = lax.axis_index("seq")
    col_index = lax.axis_index("col")
    row_index = lax.axis_index("row")
    block_index = lax.axis_index(("seq", "col"))
    own_count = hidden_in.shape[0]
    block_start = seq_index * own_count
    pieces = [hidden_in.reshape(-1), w_query.reshape(-1), w_keyval.reshape(-1)]
    bounds = [0]
    for piece in pieces:
        bounds.append(bounds[-1] + piece.shape[0])
    packed = lax.all_gather(jnp.concatenate(pieces), "seq", axis=0, tiled=False)
    shards = packed.shape[0]
    every_row = packed[:, bounds[0] : bounds[1]].reshape((-1,) + hidden_in.shape[1:])
    w_query_all = packed[:, bounds[1] : bounds[2]].reshape((-1,) + w_query.shape[1:])
    w_keyval_all = packed[:, bounds[2] : bounds[3]].reshape((-1,) + w_keyval.shape[1:])
    w_out_all = (
        doubling_gather(w_out[None], "seq", lax.axis_size("seq"))
        .transpose(1, 0, 2)
        .reshape(w_out.shape[0], -1)
    )
    total_rows = every_row.shape[0]
    requests = total_rows // NEW
    width = every_row.shape[1]
    half = width // lax.axis_size("row")
    col_start = row_index * half
    state_in = every_row.astype(jnp.float32)
    normed_in = rms_scale(state_in, attn_gain).astype(jnp.bfloat16)
    query_cols = w_query.shape[1]
    group = query_cols // HD
    query = jnp.dot(
        normed_in,
        w_query_all,
        preferred_element_type=jnp.float32,
    )
    fresh_kv = jnp.dot(
        normed_in,
        w_keyval_all,
        preferred_element_type=jnp.float32,
    )
    fresh_kv = fresh_kv.astype(jnp.bfloat16).reshape(requests, NEW, 2, HD)
    queries = query.reshape(requests, NEW * group, HD)
    scale = HD ** (-0.5)
    length_dev = kv_cache.shape[1]
    cached = kv_cache.reshape(requests, length_dev, 2, HD)
    cached_keys = kv_cache[:, :, :HD].astype(jnp.float32)
    cached_values = kv_cache[:, :, HD:].astype(jnp.float32)
    old_scores = (
        jnp.einsum("rqd,rpd->rqp", queries, cached_keys, precision=lax.Precision.HIGHEST) * scale
    )
    positions = seq_index * length_dev + jnp.arange(length_dev, dtype=jnp.int32)
    old_mask = (positions[None, :] < cache_len[:, None])[:, None, :]
    fresh_keys = fresh_kv[:, :, 0].astype(jnp.float32)
    fresh_values = fresh_kv[:, :, 1].astype(jnp.float32)
    new_scores = (
        jnp.einsum("rqd,rud->rqu", queries, fresh_keys, precision=lax.Precision.HIGHEST) * scale
    )
    token_of = jnp.arange(NEW * group, dtype=jnp.int32) // group
    new_mask = (
        (token_of[:, None] >= jnp.arange(NEW, dtype=jnp.int32)[None, :]) & (seq_index == 0)
    )[None]
    old_scores = jnp.where(old_mask, old_scores, NEG_LARGE)
    new_scores = jnp.where(new_mask, new_scores, NEG_LARGE)
    highest = jnp.maximum(jnp.max(old_scores, axis=-1), jnp.max(new_scores, axis=-1))
    old_weights = jnp.where(old_mask, jnp.exp(old_scores - highest[..., None]), 0.0)
    new_weights = jnp.where(new_mask, jnp.exp(new_scores - highest[..., None]), 0.0)
    totals = old_weights.sum(-1) + new_weights.sum(-1)
    mixed = jnp.einsum("rqp,rpd->rqd", old_weights, cached_values, precision=lax.Precision.HIGHEST)
    mixed = mixed + jnp.einsum(
        "rqu,rud->rqd", new_weights, fresh_values, precision=lax.Precision.HIGHEST
    )
    highest, totals, mixed = halving_merge(
        (highest, totals, mixed.reshape(requests, -1)), "seq", seq_count, merge_softmax
    )
    own_requests = requests // seq_count
    attended = mixed.reshape(own_requests, NEW * group, HD) / totals[..., None]
    attn_mix = attended.reshape(own_count, query_cols).astype(jnp.bfloat16)
    partial_out = jnp.dot(
        attn_mix,
        w_out_all,
        preferred_element_type=jnp.float32,
    )
    own_mid = hidden_in.astype(jnp.float32) + butterfly_sum(
        partial_out, ("row", "col"), lax.axis_size("row") * lax.axis_size("col")
    )
    own_normed = rms_scale(own_mid, ffn_gain).astype(jnp.bfloat16)
    normed_mid = doubling_gather(own_normed, "seq", seq_count)
    router = jnp.dot(normed_mid.astype(jnp.float32), w_router, precision=lax.Precision.HIGHEST)
    chosen = jnp.take_along_axis(router, routes, axis=1)
    probs = jax.nn.sigmoid(chosen - chosen[:, ::-1])
    capacity = 2 * total_rows * TOP // (EXP_DEV * seq_count)
    row_ids = jnp.arange(total_rows, dtype=jnp.int32)
    slot_ids = jnp.arange(capacity, dtype=jnp.int32)
    expert = seq_index * EXP_DEV + 0
    member = routes == expert
    in_row = jnp.any(member, axis=1)
    weight_row = jnp.sum(jnp.where(member, probs, 0.0), axis=1)
    ordering = jnp.cumsum(in_row.astype(jnp.int32)) - 1
    filled = jnp.sum(in_row.astype(jnp.int32))
    source = (
        jnp.zeros((capacity,), jnp.int32)
        .at[jnp.where(in_row, ordering, capacity)]
        .set(row_ids, mode="drop")
    )
    source_list = [source]
    weight_list = [jnp.where(slot_ids < filled, weight_row[source], 0.0)]
    source_all = jnp.stack(source_list)
    weight_all = jnp.stack(weight_list)
    normed_half = lax.dynamic_slice_in_dim(normed_mid, col_start, half, 1)
    expert_rows = normed_half[source_all]
    gate_part = jnp.einsum(
        "ecd,edgf->ecgf", expert_rows, w_gate_up, preferred_element_type=jnp.float32
    )
    gate_both = butterfly_sum(gate_part, "row", lax.axis_size("row"))
    expert_hidden = (jax.nn.silu(gate_both[:, :, 0]) * gate_both[:, :, 1]).astype(jnp.bfloat16)
    expert_result = jnp.einsum(
        "ecf,efd->ecd", expert_hidden, w_down, preferred_element_type=jnp.float32
    )
    weighted = (expert_result * weight_all[..., None]).reshape(-1, half)
    term = jnp.zeros((total_rows, half), jnp.float32).at[source_all.reshape(-1)].add(weighted)
    block_count = seq_count * lax.axis_size("col")
    out_count = total_rows // block_count
    block_mid = lax.dynamic_slice_in_dim(
        lax.dynamic_slice_in_dim(own_mid, col_index * out_count, out_count, 0), col_start, half, 1
    )
    state_out = halving_scatter(term, ("seq", "col"), block_count) + block_mid
    layer_out = state_out.astype(jnp.bfloat16)
    gain_half = lax.dynamic_slice_in_dim(final_gain, col_start, half, 0)
    normed_block = final_scale(state_out, gain_half, width)
    normed_out = doubling_gather(normed_block, ("seq", "col"), block_count)
    vocab_dev = w_head.shape[1]
    row_count = total_rows // lax.axis_size("row")
    logits = halving_scatter(
        jnp.dot(normed_out, w_head, preferred_element_type=jnp.float32),
        "row",
        lax.axis_size("row"),
    )
    own_targets = lax.dynamic_slice_in_dim(targets, row_index * row_count, row_count, 0)
    vocab_start = block_index * vocab_dev
    matches = (
        own_targets[:, None] == (vocab_start + jnp.arange(vocab_dev, dtype=jnp.int32))[None, :]
    )
    picked_local = jnp.sum(jnp.where(matches, logits, 0.0), axis=1)
    local_high = jnp.max(logits, axis=1)
    local_total = jnp.sum(jnp.exp(logits - local_high[:, None]), axis=1)
    row_high, row_total, picked = butterfly_merge(
        (local_high[None], local_total[None], picked_local[None]),
        ("seq", "col"),
        seq_count * lax.axis_size("col"),
        merge_logsumexp,
    )
    row_high, row_total, picked = row_high[0], row_total[0], picked[0]
    logprob_part = picked - (row_high + jnp.log(row_total))
    logprob = lax.all_gather(logprob_part, "row", axis=0, tiled=True)
    return (layer_out, logprob)


def solution(mesh):
    return jax.shard_map(
        on_device,
        mesh=mesh,
        in_specs=(
            P("seq", None),
            P(),
            P("seq", ("row", "col")),
            P("seq", ("row", "col")),
            P(("row", "col"), "seq"),
            P(None, "seq", ("row", "col")),
            P(),
            P(),
            P(),
            P(),
            P("seq", "row", None, "col"),
            P("seq", "col", "row"),
            P(),
            P("row", ("seq", "col")),
            P(),
        ),
        out_specs=(P(("seq", "col"), "row"), P()),
        check_vma=False,
    )
```

```python
import jax
import jax.numpy as jnp
from jax import lax
from jax.sharding import PartitionSpec as P

HD = 64
EXP_DEV = 1
TOP = 2
NEW = 4


EPSILON = 1e-05
NEG_LARGE = -1e30


def combined_all(shard, axis, combine):
    everything = jax.tree.map(lambda part: lax.all_gather(part, axis), shard)
    initial = jax.tree.map(lambda part: part[0], everything)

    def lap(k, so_far):
        return combine(so_far, jax.tree.map(lambda part: part[k], everything))

    return lax.fori_loop(1, lax.axis_size(axis), lap, initial)


def radices_of(axes):
    names = (axes,) if isinstance(axes, str) else tuple(axes)
    radices = []
    for name in reversed(names):
        size = lax.axis_size(name)
        while size > 1:
            radix = 4 if size % 4 == 0 else 2
            radices.append(radix)
            size //= radix
    return radices


def group_exchange(value, axes, stride, radix, count, chunks=None):
    digit = (lax.axis_index(axes) // stride) % radix
    received = [value if chunks is None else chunks(digit)]
    for offset in range(1, radix):
        pairs = []
        for i in range(count):
            own = (i // stride) % radix
            pairs.append((i, i + ((own + offset) % radix - own) * stride))
        sent = value if chunks is None else chunks((digit + offset) % radix)
        received.append(lax.ppermute(sent, axes, pairs))
    ordered = []
    for source in range(radix):
        offset = (digit - source) % radix
        picked = received[0]
        for other in range(1, radix):
            picked = jnp.where(offset == other, received[other], picked)
        ordered.append(picked)
    return ordered


def fold(parts, combine):
    while len(parts) > 1:
        parts = [combine(parts[i], parts[i + 1]) for i in range(0, len(parts), 2)]
    return parts[0]


def packer(value):
    edges = [0]
    for part in value:
        edges.append(edges[-1] + part.shape[-1])

    def split(packed):
        return tuple(packed[..., edges[i] : edges[i + 1]] for i in range(len(value)))

    def combine_with(combine):
        return lambda a, b: jnp.concatenate(combine(split(a), split(b)), axis=-1)

    return jnp.concatenate(value, axis=-1), split, combine_with


def butterfly_merge(value, axes, count, combine):
    packed, split, combine_with = packer(value)
    stride = 1
    for radix in radices_of(axes):
        packed = fold(group_exchange(packed, axes, stride, radix, count), combine_with(combine))
        stride *= radix
    return split(packed)


def scatter_steps(packed, axes, count, joined):
    radices = radices_of(axes)
    strides = [1]
    for radix in radices:
        strides.append(strides[-1] * radix)
    for position in reversed(range(len(radices))):
        radix = radices[position]
        size = packed.shape[0] // radix
        whole = packed
        chunks = lambda k, whole=whole, size=size: lax.dynamic_slice_in_dim(whole, k * size, size, 0)
        parts = group_exchange(whole, axes, strides[position], radix, count, chunks)
        packed = fold(parts, joined)
    return packed


def halving_merge(value, axes, count, combine):
    packed, split, combine_with = packer(value)
    return split(scatter_steps(packed, axes, count, combine_with(combine)))


def butterfly_sum(value, axes, count):
    stride = 1
    for radix in radices_of(axes):
        value = fold(group_exchange(value, axes, stride, radix, count), lambda a, b: a + b)
        stride *= radix
    return value


def halving_scatter(value, axes, count):
    return scatter_steps(value, axes, count, lambda a, b: a + b)


def doubling_gather(value, axes, count):
    stride = 1
    for radix in radices_of(axes):
        value = jnp.concatenate(group_exchange(value, axes, stride, radix, count), axis=0)
        stride *= radix
    return value


def merge_logsumexp(first, second):
    high_a, sums_a, picked_a = first
    high_b, sums_b, picked_b = second
    highest = jnp.maximum(high_a, high_b)
    return (
        highest,
        sums_a * jnp.exp(high_a - highest) + sums_b * jnp.exp(high_b - highest),
        picked_a + picked_b,
    )


def rms_scale(values, gain):
    mean_square = jnp.mean(values * values, axis=-1, keepdims=True)
    return values * lax.rsqrt(mean_square + EPSILON) * gain


def final_scale(state, gain_half, width):
    squares = lax.psum(jnp.sum(state * state, axis=-1), "row")
    return (state * lax.rsqrt(squares[:, None] / width + EPSILON) * gain_half).astype(jnp.bfloat16)


def merge_softmax(first, second):
    high_a, sums_a, mixed_a = first
    high_b, sums_b, mixed_b = second
    highest = jnp.maximum(high_a, high_b)
    factor_a = jnp.exp(high_a - highest)
    factor_b = jnp.exp(high_b - highest)
    shaped_a = mixed_a.reshape(highest.shape + (-1,)) * factor_a[..., None]
    shaped_b = mixed_b.reshape(highest.shape + (-1,)) * factor_b[..., None]
    return (
        highest,
        sums_a * factor_a + sums_b * factor_b,
        (shaped_a + shaped_b).reshape(mixed_a.shape),
    )


def on_device(
    hidden_in,
    attn_gain,
    w_query,
    w_keyval,
    w_out,
    kv_cache,
    cache_len,
    ffn_gain,
    w_router,
    routes,
    w_gate_up,
    w_down,
    final_gain,
    w_head,
    targets,
):
    seq_count = lax.axis_size("seq")
    seq_index = lax.axis_index("seq")
    col_index = lax.axis_index("col")
    row_index = lax.axis_index("row")
    block_index = lax.axis_index(("seq", "col"))
    own_count = hidden_in.shape[0]
    block_start = seq_index * own_count
    pieces = [hidden_in.reshape(-1), jnp.concatenate([w_query, w_keyval], axis=1).reshape(-1)]
    bounds = [0]
    for piece in pieces:
        bounds.append(bounds[-1] + piece.shape[0])
    packed = lax.all_gather(jnp.concatenate(pieces), "seq", axis=0, tiled=False)
    shards = packed.shape[0]
    every_row = packed[:, bounds[0] : bounds[1]].reshape((-1,) + hidden_in.shape[1:])
    w_both_all = packed[:, bounds[1] : bounds[2]].reshape(-1, w_query.shape[1] + w_keyval.shape[1])
    w_out_all = (
        doubling_gather(w_out[None], "seq", lax.axis_size("seq"))
        .transpose(1, 0, 2)
        .reshape(w_out.shape[0], -1)
    )
    total_rows = every_row.shape[0]
    requests = total_rows // NEW
    width = every_row.shape[1]
    half = width // lax.axis_size("row")
    col_start = row_index * half
    state_in = every_row.astype(jnp.float32)
    normed_in = rms_scale(state_in, attn_gain).astype(jnp.bfloat16)
    query_cols = w_query.shape[1]
    group = query_cols // HD
    both = jnp.dot(normed_in, w_both_all, preferred_element_type=jnp.float32)
    query = both[:, : w_query.shape[1]]
    fresh_kv = both[:, w_query.shape[1] :]
    fresh_kv = fresh_kv.astype(jnp.bfloat16).reshape(requests, NEW, 2, HD)
    queries = query.reshape(requests, NEW * group, HD)
    scale = HD ** (-0.5)
    length_dev = kv_cache.shape[1]
    cached = kv_cache.reshape(requests, length_dev, 2, HD)
    cached_keys = cached[:, :, 0].astype(jnp.float32)
    cached_values = cached[:, :, 1].astype(jnp.float32)
    old_scores = (
        jnp.einsum("rqd,rpd->rqp", queries, cached_keys, precision=lax.Precision.HIGHEST) * scale
    )
    positions = seq_index * length_dev + jnp.arange(length_dev, dtype=jnp.int32)
    old_mask = (positions[None, :] < cache_len[:, None])[:, None, :]
    fresh_keys = fresh_kv[:, :, 0].astype(jnp.float32)
    fresh_values = fresh_kv[:, :, 1].astype(jnp.float32)
    new_scores = (
        jnp.einsum("rqd,rud->rqu", queries, fresh_keys, precision=lax.Precision.HIGHEST) * scale
    )
    token_of = jnp.arange(NEW * group, dtype=jnp.int32) // group
    new_mask = (
        (token_of[:, None] >= jnp.arange(NEW, dtype=jnp.int32)[None, :]) & (seq_index == 0)
    )[None]
    old_scores = jnp.where(old_mask, old_scores, NEG_LARGE)
    new_scores = jnp.where(new_mask, new_scores, NEG_LARGE)
    highest = jnp.maximum(jnp.max(old_scores, axis=-1), jnp.max(new_scores, axis=-1))
    old_weights = jnp.where(old_mask, jnp.exp(old_scores - highest[..., None]), 0.0)
    new_weights = jnp.where(new_mask, jnp.exp(new_scores - highest[..., None]), 0.0)
    totals = old_weights.sum(-1) + new_weights.sum(-1)
    mixed = jnp.einsum("rqp,rpd->rqd", old_weights, cached_values, precision=lax.Precision.HIGHEST)
    mixed = mixed + jnp.einsum(
        "rqu,rud->rqd", new_weights, fresh_values, precision=lax.Precision.HIGHEST
    )
    highest, totals, mixed = halving_merge(
        (highest, totals, mixed.reshape(requests, -1)), "seq", seq_count, merge_softmax
    )
    own_requests = requests // seq_count
    attended = mixed.reshape(own_requests, NEW * group, HD) / totals[..., None]
    attn_mix = attended.reshape(own_count, query_cols).astype(jnp.bfloat16)
    partial_out = jnp.dot(
        attn_mix,
        w_out_all,
        preferred_element_type=jnp.float32,
    )
    own_mid = hidden_in.astype(jnp.float32) + butterfly_sum(
        partial_out, ("row", "col"), lax.axis_size("row") * lax.axis_size("col")
    )
    own_normed = rms_scale(own_mid, ffn_gain).astype(jnp.bfloat16)
    normed_mid = doubling_gather(own_normed, "seq", seq_count)
    router = jnp.dot(normed_mid.astype(jnp.float32), w_router, precision=lax.Precision.HIGHEST)
    chosen = jnp.take_along_axis(router, routes, axis=1)
    probs = jax.nn.sigmoid(chosen - chosen[:, ::-1])
    capacity = 2 * total_rows * TOP // (EXP_DEV * seq_count)
    row_ids = jnp.arange(total_rows, dtype=jnp.int32)
    slot_ids = jnp.arange(capacity, dtype=jnp.int32)
    expert = seq_index * EXP_DEV + 0
    member = routes == expert
    in_row = jnp.any(member, axis=1)
    weight_row = jnp.sum(jnp.where(member, probs, 0.0), axis=1)
    ordering = jnp.cumsum(in_row.astype(jnp.int32)) - 1
    filled = jnp.sum(in_row.astype(jnp.int32))
    source = (
        jnp.zeros((capacity,), jnp.int32)
        .at[jnp.where(in_row, ordering, capacity)]
        .set(row_ids, mode="drop")
    )
    source_list = [source]
    weight_list = [jnp.where(slot_ids < filled, weight_row[source], 0.0)]
    source_all = jnp.stack(source_list)
    weight_all = jnp.stack(weight_list)
    normed_half = lax.dynamic_slice_in_dim(normed_mid, col_start, half, 1)
    expert_rows = normed_half[source_all]
    gate_part = jnp.einsum(
        "ecd,edgf->ecgf", expert_rows, w_gate_up, preferred_element_type=jnp.float32
    )
    gate_both = butterfly_sum(gate_part, "row", lax.axis_size("row"))
    expert_hidden = (jax.nn.silu(gate_both[:, :, 0]) * gate_both[:, :, 1]).astype(jnp.bfloat16)
    expert_result = jnp.einsum(
        "ecf,efd->ecd", expert_hidden, w_down, preferred_element_type=jnp.float32
    )
    weighted = (expert_result * weight_all[..., None]).reshape(-1, half)
    term = jnp.zeros((total_rows, half), jnp.float32).at[source_all.reshape(-1)].add(weighted)
    block_count = seq_count * lax.axis_size("col")
    out_count = total_rows // block_count
    block_mid = lax.dynamic_slice_in_dim(
        lax.dynamic_slice_in_dim(own_mid, col_index * out_count, out_count, 0), col_start, half, 1
    )
    state_out = halving_scatter(term, ("seq", "col"), block_count) + block_mid
    layer_out = state_out.astype(jnp.bfloat16)
    gain_half = lax.dynamic_slice_in_dim(final_gain, col_start, half, 0)
    normed_block = final_scale(state_out, gain_half, width)
    normed_out = doubling_gather(normed_block, ("seq", "col"), block_count)
    vocab_dev = w_head.shape[1]
    row_count = total_rows // lax.axis_size("row")
    logits = halving_scatter(
        jnp.dot(normed_out, w_head, preferred_element_type=jnp.float32),
        "row",
        lax.axis_size("row"),
    )
    own_targets = lax.dynamic_slice_in_dim(targets, row_index * row_count, row_count, 0)
    vocab_start = block_index * vocab_dev
    matches = (
        own_targets[:, None] == (vocab_start + jnp.arange(vocab_dev, dtype=jnp.int32))[None, :]
    )
    picked_local = jnp.sum(jnp.where(matches, logits, 0.0), axis=1)
    local_high = jnp.max(logits, axis=1)
    local_total = jnp.sum(jnp.exp(logits - local_high[:, None]), axis=1)
    row_high, row_total, picked = butterfly_merge(
        (local_high[None], local_total[None], picked_local[None]),
        ("seq", "col"),
        seq_count * lax.axis_size("col"),
        merge_logsumexp,
    )
    row_high, row_total, picked = row_high[0], row_total[0], picked[0]
    logprob_part = picked - (row_high + jnp.log(row_total))
    logprob = lax.all_gather(logprob_part, "row", axis=0, tiled=True)
    return (layer_out, logprob)


def solution(mesh):
    return jax.shard_map(
        on_device,
        mesh=mesh,
        in_specs=(
            P("seq", None),
            P(),
            P("seq", ("row", "col")),
            P("seq", ("row", "col")),
            P(("row", "col"), "seq"),
            P(None, "seq", ("row", "col")),
            P(),
            P(),
            P(),
            P(),
            P("seq", "row", None, "col"),
            P("seq", "col", "row"),
            P(),
            P("row", ("seq", "col")),
            P(),
        ),
        out_specs=(P(("seq", "col"), "row"), P()),
        check_vma=False,
    )
```

```python
import jax
import jax.numpy as jnp
from jax import lax
from jax.sharding import PartitionSpec as P

HD = 64
EXP_DEV = 1
TOP = 2
NEW = 4


EPSILON = 1e-05
NEG_LARGE = -1e30


def combined_all(shard, axis, combine):
    everything = jax.tree.map(lambda part: lax.all_gather(part, axis), shard)
    initial = jax.tree.map(lambda part: part[0], everything)

    def lap(k, so_far):
        return combine(so_far, jax.tree.map(lambda part: part[k], everything))

    return lax.fori_loop(1, lax.axis_size(axis), lap, initial)


def radices_of(axes):
    names = (axes,) if isinstance(axes, str) else tuple(axes)
    radices = []
    for name in reversed(names):
        size = lax.axis_size(name)
        while size > 1:
            radix = 4 if size % 4 == 0 else 2
            radices.append(radix)
            size //= radix
    return radices


def group_exchange(value, axes, stride, radix, count, chunks=None):
    digit = (lax.axis_index(axes) // stride) % radix
    received = [value if chunks is None else chunks(digit)]
    for offset in range(1, radix):
        pairs = []
        for i in range(count):
            own = (i // stride) % radix
            pairs.append((i, i + ((own + offset) % radix - own) * stride))
        sent = value if chunks is None else chunks((digit + offset) % radix)
        received.append(lax.ppermute(sent, axes, pairs))
    ordered = []
    for source in range(radix):
        offset = (digit - source) % radix
        picked = received[0]
        for other in range(1, radix):
            picked = jnp.where(offset == other, received[other], picked)
        ordered.append(picked)
    return ordered


def fold(parts, combine):
    while len(parts) > 1:
        parts = [combine(parts[i], parts[i + 1]) for i in range(0, len(parts), 2)]
    return parts[0]


def packer(value):
    edges = [0]
    for part in value:
        edges.append(edges[-1] + part.shape[-1])

    def split(packed):
        return tuple(packed[..., edges[i] : edges[i + 1]] for i in range(len(value)))

    def combine_with(combine):
        return lambda a, b: jnp.concatenate(combine(split(a), split(b)), axis=-1)

    return jnp.concatenate(value, axis=-1), split, combine_with


def butterfly_merge(value, axes, count, combine):
    packed, split, combine_with = packer(value)
    stride = 1
    for radix in radices_of(axes):
        packed = fold(group_exchange(packed, axes, stride, radix, count), combine_with(combine))
        stride *= radix
    return split(packed)


def scatter_steps(packed, axes, count, joined):
    radices = radices_of(axes)
    strides = [1]
    for radix in radices:
        strides.append(strides[-1] * radix)
    for position in reversed(range(len(radices))):
        radix = radices[position]
        size = packed.shape[0] // radix
        whole = packed
        chunks = lambda k, whole=whole, size=size: lax.dynamic_slice_in_dim(whole, k * size, size, 0)
        parts = group_exchange(whole, axes, strides[position], radix, count, chunks)
        packed = fold(parts, joined)
    return packed


def halving_merge(value, axes, count, combine):
    packed, split, combine_with = packer(value)
    return split(scatter_steps(packed, axes, count, combine_with(combine)))


def butterfly_sum(value, axes, count):
    stride = 1
    for radix in radices_of(axes):
        value = fold(group_exchange(value, axes, stride, radix, count), lambda a, b: a + b)
        stride *= radix
    return value


def halving_scatter(value, axes, count):
    return scatter_steps(value, axes, count, lambda a, b: a + b)


def doubling_gather(value, axes, count):
    stride = 1
    for radix in radices_of(axes):
        value = jnp.concatenate(group_exchange(value, axes, stride, radix, count), axis=0)
        stride *= radix
    return value


def merge_logsumexp(first, second):
    high_a, sums_a, picked_a = first
    high_b, sums_b, picked_b = second
    highest = jnp.maximum(high_a, high_b)
    return (
        highest,
        sums_a * jnp.exp(high_a - highest) + sums_b * jnp.exp(high_b - highest),
        picked_a + picked_b,
    )


def rms_scale(values, gain):
    mean_square = jnp.mean(values * values, axis=-1, keepdims=True)
    return values * lax.rsqrt(mean_square + EPSILON) * gain


def final_scale(state, gain_half, width):
    squares = lax.psum(jnp.sum(state * state, axis=-1), "row")
    return (state * lax.rsqrt(squares[:, None] / width + EPSILON) * gain_half).astype(jnp.bfloat16)


def merge_softmax(first, second):
    high_a, sums_a, mixed_a = first
    high_b, sums_b, mixed_b = second
    highest = jnp.maximum(high_a, high_b)
    factor_a = jnp.exp(high_a - highest)
    factor_b = jnp.exp(high_b - highest)
    shaped_a = mixed_a.reshape(highest.shape + (-1,)) * factor_a[..., None]
    shaped_b = mixed_b.reshape(highest.shape + (-1,)) * factor_b[..., None]
    return (
        highest,
        sums_a * factor_a + sums_b * factor_b,
        (shaped_a + shaped_b).reshape(mixed_a.shape),
    )


def on_device(
    hidden_in,
    attn_gain,
    w_query,
    w_keyval,
    w_out,
    kv_cache,
    cache_len,
    ffn_gain,
    w_router,
    routes,
    w_gate_up,
    w_down,
    final_gain,
    w_head,
    targets,
):
    seq_count = lax.axis_size("seq")
    seq_index = lax.axis_index("seq")
    col_index = lax.axis_index("col")
    row_index = lax.axis_index("row")
    block_index = lax.axis_index(("seq", "col"))
    own_count = hidden_in.shape[0]
    block_start = seq_index * own_count
    own_normed_in = rms_scale(hidden_in.astype(jnp.float32), attn_gain).astype(jnp.bfloat16)
    pieces = [own_normed_in.reshape(-1), jnp.concatenate([w_query, w_keyval], axis=1).reshape(-1)]
    bounds = [0]
    for piece in pieces:
        bounds.append(bounds[-1] + piece.shape[0])
    packed = lax.all_gather(jnp.concatenate(pieces), "seq", axis=0, tiled=False)
    shards = packed.shape[0]
    every_row = packed[:, bounds[0] : bounds[1]].reshape((-1,) + hidden_in.shape[1:])
    w_both_all = packed[:, bounds[1] : bounds[2]].reshape(-1, w_query.shape[1] + w_keyval.shape[1])
    w_out_all = (
        doubling_gather(w_out[None], "seq", lax.axis_size("seq"))
        .transpose(1, 0, 2)
        .reshape(w_out.shape[0], -1)
    )
    total_rows = every_row.shape[0]
    requests = total_rows // NEW
    width = every_row.shape[1]
    half = width // lax.axis_size("row")
    col_start = row_index * half
    normed_in = every_row
    query_cols = w_query.shape[1]
    group = query_cols // HD
    both = jnp.dot(normed_in, w_both_all, preferred_element_type=jnp.float32)
    query = both[:, : w_query.shape[1]]
    fresh_kv = both[:, w_query.shape[1] :]
    fresh_kv = fresh_kv.astype(jnp.bfloat16).reshape(requests, NEW, 2, HD)
    queries = query.reshape(requests, NEW * group, HD)
    scale = HD ** (-0.5)
    length_dev = kv_cache.shape[1]
    cached = kv_cache.reshape(requests, length_dev, 2, HD)
    cached_keys = cached[:, :, 0].astype(jnp.float32)
    cached_values = cached[:, :, 1].astype(jnp.float32)
    old_scores = (
        jnp.einsum("rqd,rpd->rqp", queries, cached_keys, precision=lax.Precision.HIGHEST) * scale
    )
    positions = seq_index * length_dev + jnp.arange(length_dev, dtype=jnp.int32)
    old_mask = (positions[None, :] < cache_len[:, None])[:, None, :]
    fresh_keys = fresh_kv[:, :, 0].astype(jnp.float32)
    fresh_values = fresh_kv[:, :, 1].astype(jnp.float32)
    new_scores = (
        jnp.einsum("rqd,rud->rqu", queries, fresh_keys, precision=lax.Precision.HIGHEST) * scale
    )
    token_of = jnp.arange(NEW * group, dtype=jnp.int32) // group
    new_mask = (
        (token_of[:, None] >= jnp.arange(NEW, dtype=jnp.int32)[None, :]) & (seq_index == 0)
    )[None]
    old_scores = jnp.where(old_mask, old_scores, NEG_LARGE)
    new_scores = jnp.where(new_mask, new_scores, NEG_LARGE)
    highest = jnp.maximum(jnp.max(old_scores, axis=-1), jnp.max(new_scores, axis=-1))
    old_weights = jnp.where(old_mask, jnp.exp(old_scores - highest[..., None]), 0.0)
    new_weights = jnp.where(new_mask, jnp.exp(new_scores - highest[..., None]), 0.0)
    totals = old_weights.sum(-1) + new_weights.sum(-1)
    mixed = jnp.einsum("rqp,rpd->rqd", old_weights, cached_values, precision=lax.Precision.HIGHEST)
    mixed = mixed + jnp.einsum(
        "rqu,rud->rqd", new_weights, fresh_values, precision=lax.Precision.HIGHEST
    )
    highest, totals, mixed = halving_merge(
        (highest, totals, mixed.reshape(requests, -1)), "seq", seq_count, merge_softmax
    )
    own_requests = requests // seq_count
    attended = mixed.reshape(own_requests, NEW * group, HD) / totals[..., None]
    attn_mix = attended.reshape(own_count, query_cols).astype(jnp.bfloat16)
    partial_out = jnp.dot(
        attn_mix,
        w_out_all,
        preferred_element_type=jnp.float32,
    )
    own_mid = hidden_in.astype(jnp.float32) + butterfly_sum(
        partial_out, ("row", "col"), lax.axis_size("row") * lax.axis_size("col")
    )
    own_normed = rms_scale(own_mid, ffn_gain).astype(jnp.bfloat16)
    normed_mid = doubling_gather(own_normed, "seq", seq_count)
    router = jnp.dot(normed_mid.astype(jnp.float32), w_router, precision=lax.Precision.HIGHEST)
    chosen = jnp.take_along_axis(router, routes, axis=1)
    probs = jax.nn.sigmoid(chosen - chosen[:, ::-1])
    capacity = 2 * total_rows * TOP // (EXP_DEV * seq_count)
    row_ids = jnp.arange(total_rows, dtype=jnp.int32)
    slot_ids = jnp.arange(capacity, dtype=jnp.int32)
    expert = seq_index * EXP_DEV + 0
    member = routes == expert
    in_row = jnp.any(member, axis=1)
    weight_row = jnp.sum(jnp.where(member, probs, 0.0), axis=1)
    ordering = jnp.cumsum(in_row.astype(jnp.int32)) - 1
    filled = jnp.sum(in_row.astype(jnp.int32))
    source = (
        jnp.zeros((capacity,), jnp.int32)
        .at[jnp.where(in_row, ordering, capacity)]
        .set(row_ids, mode="drop")
    )
    source_list = [source]
    weight_list = [jnp.where(slot_ids < filled, weight_row[source], 0.0)]
    source_all = jnp.stack(source_list)
    weight_all = jnp.stack(weight_list)
    normed_half = lax.dynamic_slice_in_dim(normed_mid, col_start, half, 1)
    expert_rows = normed_half[source_all]
    gate_part = jnp.einsum(
        "ecd,edgf->ecgf", expert_rows, w_gate_up, preferred_element_type=jnp.float32
    )
    gate_both = butterfly_sum(gate_part, "row", lax.axis_size("row"))
    expert_hidden = (jax.nn.silu(gate_both[:, :, 0]) * gate_both[:, :, 1]).astype(jnp.bfloat16)
    expert_result = jnp.einsum(
        "ecf,efd->ecd", expert_hidden, w_down, preferred_element_type=jnp.float32
    )
    weighted = (expert_result * weight_all[..., None]).reshape(-1, half)
    term = jnp.zeros((total_rows, half), jnp.float32).at[source_all.reshape(-1)].add(weighted)
    block_count = seq_count * lax.axis_size("col")
    out_count = total_rows // block_count
    block_mid = lax.dynamic_slice_in_dim(
        lax.dynamic_slice_in_dim(own_mid, col_index * out_count, out_count, 0), col_start, half, 1
    )
    state_out = halving_scatter(term, ("seq", "col"), block_count) + block_mid
    layer_out = state_out.astype(jnp.bfloat16)
    gain_half = lax.dynamic_slice_in_dim(final_gain, col_start, half, 0)
    normed_block = final_scale(state_out, gain_half, width)
    normed_out = doubling_gather(normed_block, ("seq", "col"), block_count)
    vocab_dev = w_head.shape[1]
    row_count = total_rows // lax.axis_size("row")
    logits = halving_scatter(
        jnp.dot(normed_out, w_head, preferred_element_type=jnp.float32),
        "row",
        lax.axis_size("row"),
    )
    own_targets = lax.dynamic_slice_in_dim(targets, row_index * row_count, row_count, 0)
    vocab_start = block_index * vocab_dev
    matches = (
        own_targets[:, None] == (vocab_start + jnp.arange(vocab_dev, dtype=jnp.int32))[None, :]
    )
    picked_local = jnp.sum(jnp.where(matches, logits, 0.0), axis=1)
    local_high = jnp.max(logits, axis=1)
    local_total = jnp.sum(jnp.exp(logits - local_high[:, None]), axis=1)
    row_high, row_total, picked = butterfly_merge(
        (local_high[None], local_total[None], picked_local[None]),
        ("seq", "col"),
        seq_count * lax.axis_size("col"),
        merge_logsumexp,
    )
    row_high, row_total, picked = row_high[0], row_total[0], picked[0]
    logprob_part = picked - (row_high + jnp.log(row_total))
    logprob = lax.all_gather(logprob_part, "row", axis=0, tiled=True)
    return (layer_out, logprob)


def solution(mesh):
    return jax.shard_map(
        on_device,
        mesh=mesh,
        in_specs=(
            P("seq", None),
            P(),
            P("seq", ("row", "col")),
            P("seq", ("row", "col")),
            P(("row", "col"), "seq"),
            P(None, "seq", ("row", "col")),
            P(),
            P(),
            P(),
            P(),
            P("seq", "row", None, "col"),
            P("seq", "col", "row"),
            P(),
            P("row", ("seq", "col")),
            P(),
        ),
        out_specs=(P(("seq", "col"), "row"), P()),
        check_vma=False,
    )
```
